512 devices in a mesh: ep: 128 (over z, y, core), dp: 4 (over x).
Axes of the slice: x: 4, y: 8, z: 8, core: 2. Of those that a mesh axis runs over, the one named last changes fastest.
Arguments:
- tokens: bfloat16 [8192, 2048], P('ep', 'dp'), may hold values from -6 to 6
- expert_ids: int32 [8192, 8], P('ep'), may hold values from 0 to 127, as said below
- gate_probs: float32 [8192, 8], P('ep'), may hold values from 0.05 to 1
- gate_weight: bfloat16 [128, 2048, 1024], P('ep', None, 'dp'), may hold values from -0.125 to 0.125
- up_weight: bfloat16 [128, 2048, 1024], P('ep', None, 'dp'), may hold values from -0.125 to 0.125
- down_weight: bfloat16 [128, 1024, 2048], P('ep', None, 'dp'), may hold values from -0.1875 to 0.1875
Outputs:
- combined: bfloat16 [8192, 2048], P('ep', 'dp')
The draws below stay inside these ranges and needn't reach their ends.
Inputs may be any that keep to these rules, and one draw needn't show every extreme that they name: `expert_ids`: each row names 8 different experts. The same 2 experts, the same pair on every device, are each named exactly 16 times among the 64 rows of each device, and every other expert at most 4 times among a device's rows, some exactly 4 times.
All inputs are finite; a program needn't handle non-finite values.
Results may differ from the reference program's by a relative error of at most 0.0057.
Values may be sent and summed in bfloat16 or wider, within the bound.
No kernel may reach another device: no remote copies, remote signals or barrier semaphores. Data moves between devices by JAX's collectives and lax.ppermute only.
A program may use at most 64 MiB of HBM per device.

```python
import jax
import jax.numpy as jnp
from jax import lax

D = 2048
FF = 1024
TOPK = 8
HOT = 2
TOK_DEV = 64
EXPERTS = 128
TOKENS = 8192
HOTLOAD = 16
CAP = 4
N_EP = 128


def draw_expert_ids(key, part):
    cold_count = EXPERTS - HOT
    blocks_count = TOKENS // TOK_DEV
    ordering = jax.random.permutation(jax.random.fold_in(key, 11), EXPERTS).astype(jnp.int32)
    hot_ids = ordering[:HOT]
    cold_ids = ordering[HOT:]
    rank_range = jnp.arange(TOK_DEV, dtype=jnp.int32)
    column = jnp.arange(TOPK, dtype=jnp.int32)
    offsets = jnp.arange(HOT, dtype=jnp.int32) * (TOK_DEV // HOT)
    flags = ((rank_range[:, None] - offsets[None, :]) % TOK_DEV < HOTLOAD).astype(jnp.int32)
    hot_number = jnp.sum(flags, axis=1)
    cold_number = TOPK - hot_number
    cold_start = jnp.cumsum(cold_number) - cold_number
    hot_before = jnp.cumsum(flags, axis=1) - flags
    hot_pick = jnp.sum(flags[:, None, :] * (hot_before[:, None, :] == column[None, :, None]).astype(jnp.int32) * hot_ids[None, None, :], axis=2)
    cold_position = (cold_start[:, None] + column[None, :] - hot_number[:, None]) % cold_count
    rotation = (column[None, :] + rank_range[:, None]) % TOPK

    def one_block(block):
        block_key = jax.random.fold_in(key, 100 + block)
        cold_order = jax.random.permutation(jax.random.fold_in(block_key, 1), cold_count).astype(jnp.int32)
        block_cold = cold_ids[cold_order]
        token_rank = jax.random.permutation(jax.random.fold_in(block_key, 2), TOK_DEV).astype(jnp.int32)
        cold_pick = block_cold[cold_position]
        by_rank = jnp.where(column[None, :] < hot_number[:, None], hot_pick, cold_pick)
        by_rank = jnp.take_along_axis(by_rank, rotation, axis=1)
        return by_rank[token_rank]
    blocks = lax.map(one_block, jnp.arange(blocks_count, dtype=jnp.int32))
    return blocks.reshape(TOKENS, TOPK).astype(jnp.int32)


def level_of(key, dims, cuts, smallest, largest):
    def one(axis_at, shards_of):
        steps = jax.random.uniform(jax.random.fold_in(jax.random.fold_in(key, 6), axis_at), (shards_of,), jnp.float32, smallest / len(cuts), largest / len(cuts))
        return jnp.repeat(jnp.exp(steps), dims[axis_at] // shards_of).reshape((-1,) + (1,) * (len(dims) - axis_at - 1))

    loudness = one(*cuts[0])
    for cut in cuts[1:]:
        loudness = loudness * one(*cut)
    return loudness


def noise(own_key, extent, spread, most, cuts=(), kind=jnp.bfloat16):
    array = spread * jax.random.normal(own_key, extent, jnp.float32)
    if cuts:
        array = array * level_of(own_key, extent, cuts, -0.22, 0.18)
    return jnp.clip(array, -most, most).astype(kind)


def setup_inputs(seed: int = 0) -> dict:
    streams_of = jax.random.split(jax.random.key(seed), 7)
    tokens = noise(streams_of[0], (TOKENS, D), 1.0, 6.0, ((0, 128), (1, 4)))
    expert_ids = draw_expert_ids(jax.random.fold_in(streams_of[6], 71), 0)
    gate_probs = jnp.clip(0.05 + 0.95 * jax.random.uniform(streams_of[2], (TOKENS, TOPK), jnp.float32) ** level_of(streams_of[2], (TOKENS, TOPK), ((0, 128),), -0.2, 0.2), 0.05, 1.0)
    gate_weight = noise(streams_of[3], (EXPERTS, D, FF), D ** -0.5, 0.125, ((0, 128), (2, 4)))
    up_weight = noise(streams_of[4], (EXPERTS, D, FF), D ** -0.5, 0.125, ((0, 128), (2, 4)))
    down_weight = noise(streams_of[5], (EXPERTS, FF, D), FF ** -0.5, 0.1875, ((0, 128), (2, 4)))
    return {"tokens": tokens, "expert_ids": expert_ids, "gate_probs": gate_probs, "gate_weight": gate_weight, "up_weight": up_weight, "down_weight": down_weight}


def expert_apply(gathered, w_gate, w_up, w_down):
    gate_part = jnp.dot(gathered, w_gate, preferred_element_type=jnp.float32)
    up_part = jnp.dot(gathered, w_up, preferred_element_type=jnp.float32)
    hidden = (jax.nn.silu(gate_part) * up_part).astype(jnp.bfloat16)
    return jnp.dot(hidden, w_down, preferred_element_type=jnp.float32).astype(jnp.bfloat16)


def reference(tokens, expert_ids, gate_probs, gate_weight, up_weight, down_weight):
    expert_count = gate_weight.shape[0]
    flat_ids = expert_ids.reshape(-1).astype(jnp.int32)
    flat_probs = gate_probs.reshape(-1)
    assignments = flat_ids.shape[0]
    expert_range = jnp.arange(expert_count, dtype=jnp.int32)
    expert_loads = jnp.zeros((expert_count,), jnp.int32).at[flat_ids].add(1)
    scores = expert_loads * expert_count + (expert_count - 1 - expert_range)
    _, hot_ids = lax.top_k(scores, HOT)
    hot_ids = hot_ids.astype(jnp.int32)
    hot_flag = jnp.zeros((expert_count,), jnp.int32).at[hot_ids].set(1)

    def add_expert(accum, expert, row_limit, allowed):
        selected = (flat_ids == expert) & allowed
        picked = jnp.nonzero(selected, size=row_limit, fill_value=assignments)[0].astype(jnp.int32)
        token_index = (picked // TOPK).astype(jnp.int32)
        gathered = jnp.take(tokens, token_index, axis=0, mode="fill", fill_value=0)
        result = expert_apply(gathered, gate_weight[expert], up_weight[expert], down_weight[expert])
        weights = jnp.take(flat_probs, picked, mode="fill", fill_value=0)
        return accum.at[token_index].add(weights[:, None] * result.astype(jnp.float32), mode="drop")

    def cold_step(accum, expert):
        allowed = hot_flag[expert] == 0
        return add_expert(accum, expert, N_EP * CAP, allowed), None

    def hot_step(accum, expert):
        return add_expert(accum, expert, N_EP * HOTLOAD, True), None

    accum = jnp.zeros((tokens.shape[0], tokens.shape[1]), jnp.float32)
    accum, _ = lax.scan(cold_step, accum, expert_range)
    accum, _ = lax.scan(hot_step, accum, hot_ids)
    return accum.astype(jnp.bfloat16)
```

```python
import math

import jax
import jax.numpy as jnp
from jax import lax
from jax.sharding import Mesh
from jax.sharding import PartitionSpec as P

HOT = 2
EP = ("eph", "c")


def silu_product(gate_part, up_part):
    return (jax.nn.silu(gate_part) * up_part).astype(jnp.bfloat16)


def local(tokens, expert_ids, gate_probs, gate_weight, up_weight, down_weight):
    pair_count = lax.axis_size("eph")
    ep_count = pair_count * HOT
    dp_count = lax.axis_size("dp")
    parity = lax.axis_index("c")
    ep_index = lax.axis_index("eph") * HOT + parity
    tok_rows, top_count = expert_ids.shape
    exp_dev = gate_weight.shape[0]
    expert_count = exp_dev * ep_count
    hot_load = min(tok_rows * 3 // 4, 4 * tok_rows * top_count // expert_count)
    cold_total = tok_rows * top_count - HOT * hot_load
    capacity = (cold_total + expert_count - HOT - 1) // (expert_count - HOT)
    host_count = pair_count
    spare_slots = max(1, math.ceil(hot_load / host_count))
    primary_slots = exp_dev * capacity

    flat_ids = expert_ids.reshape(-1)
    expert_range = jnp.arange(expert_count, dtype=jnp.int32)
    matches = (flat_ids[:, None] == expert_range[None, :]).astype(jnp.int32)
    expert_loads = jnp.sum(matches, axis=0)
    _, hot_ids = lax.top_k(expert_loads * expert_count + (expert_count - 1 - expert_range), HOT)

    own = (gate_weight[0], up_weight[0], down_weight[0])
    swapped = tuple(lax.ppermute(w, "c", [(0, 1), (1, 0)]) for w in own)
    mine = hot_ids[parity]
    my_expert = ep_index
    sibling_expert = ep_index ^ 1
    take_own = mine == my_expert
    take_sib = mine == sibling_expert
    contrib = tuple(
        jnp.where(take_own, a, jnp.where(take_sib, b, jnp.zeros_like(a)))
        for a, b in zip(own, swapped)
    )
    spare_gate, spare_up, spare_down = (lax.psum(w, "eph") for w in contrib)

    earlier = jnp.cumsum(matches, axis=0) - matches
    order_rank = jnp.sum(earlier * matches, axis=1)
    hot_match = (flat_ids[:, None] == hot_ids[None, :]).astype(jnp.int32)
    is_hot = jnp.sum(hot_match, axis=1) > 0
    which_hot = jnp.sum(hot_match * jnp.arange(HOT, dtype=jnp.int32)[None, :], axis=1)
    spread = (ep_index * hot_load + order_rank) % host_count
    hot_target = (spread * HOT + which_hot) * spare_slots + order_rank // host_count
    cold_target = (
        flat_ids // exp_dev * primary_slots + flat_ids % exp_dev * capacity + order_rank
    )
    pick_row = jnp.arange(tok_rows * top_count, dtype=jnp.int32) // top_count
    primary_total = ep_count * primary_slots
    spare_total = ep_count * spare_slots
    cold_source = jnp.full((primary_total,), tok_rows, jnp.int32)
    cold_source = cold_source.at[jnp.where(is_hot, primary_total, cold_target)].set(
        pick_row, mode="drop"
    )
    hot_source = jnp.full((spare_total,), tok_rows, jnp.int32)
    hot_source = hot_source.at[jnp.where(is_hot, hot_target, spare_total)].set(
        pick_row, mode="drop"
    )

    features = lax.all_gather(tokens, "dp", axis=1, tiled=True)
    model_width = features.shape[1]
    source_row = jnp.concatenate(
        [cold_source.reshape(ep_count, primary_slots), hot_source.reshape(ep_count, spare_slots)],
        axis=1,
    )
    outgoing = jnp.take(features, source_row, axis=0, mode="fill", fill_value=0)
    incoming = lax.all_to_all(outgoing, EP, split_axis=0, concat_axis=0, tiled=True)
    primary_rows = incoming[:, :primary_slots].reshape(ep_count, exp_dev, capacity, model_width)
    spare_rows = incoming[:, primary_slots:]

    gate_primary = jnp.einsum(
        "secd,edf->secf", primary_rows, gate_weight, preferred_element_type=jnp.float32
    )
    up_primary = jnp.einsum(
        "secd,edf->secf", primary_rows, up_weight, preferred_element_type=jnp.float32
    )
    hidden_primary = silu_product(gate_primary, up_primary)
    stacked = jnp.broadcast_to(hidden_primary[None], (dp_count,) + hidden_primary.shape)
    part_primary = lax.all_to_all(stacked, "dp", split_axis=0, concat_axis=0, tiled=True)
    feature_local = down_weight.shape[2]
    down_split = down_weight.reshape(exp_dev, dp_count, -1, feature_local)
    out_primary = jnp.einsum(
        "nsecf,enfd->secd", part_primary, down_split, preferred_element_type=jnp.float32
    ).astype(jnp.bfloat16)
    back_primary = lax.all_to_all(
        out_primary.reshape(ep_count, primary_slots, feature_local),
        EP,
        split_axis=0,
        concat_axis=0,
        tiled=True,
    ).reshape(primary_total, feature_local)

    gate_spare = jnp.einsum(
        "srd,df->srf", spare_rows, spare_gate, preferred_element_type=jnp.float32
    )
    up_spare = jnp.einsum("srd,df->srf", spare_rows, spare_up, preferred_element_type=jnp.float32)
    hidden_spare = silu_product(gate_spare, up_spare)
    part_spare = lax.all_gather(hidden_spare, "dp", axis=2, tiled=True)
    out_spare = jnp.einsum(
        "srf,fd->srd", part_spare, spare_down, preferred_element_type=jnp.float32
    ).astype(jnp.bfloat16)
    back_spare = lax.all_to_all(out_spare, EP, split_axis=0, concat_axis=0, tiled=True).reshape(
        spare_total, feature_local
    )

    returned = jnp.concatenate([back_primary, back_spare], axis=0)
    target = jnp.where(is_hot, primary_total + hot_target, cold_target)
    fetched = jnp.take(returned, target, axis=0).reshape(tok_rows, top_count, feature_local)
    combined = jnp.sum(gate_probs[:, :, None] * fetched.astype(jnp.float32), axis=1)
    return combined.astype(jnp.bfloat16)


def solution(mesh):
    ep_size, dp_size = mesh.devices.shape
    split = Mesh(mesh.devices.reshape(ep_size // HOT, HOT, dp_size), ("eph", "c", "dp"))
    in_specs = (
        P(EP, "dp"),
        P(EP, None),
        P(EP, None),
        P(EP, None, "dp"),
        P(EP, None, "dp"),
        P(EP, None, "dp"),
    )
    out_specs = P(EP, "dp")
    return jax.shard_map(local, mesh=split, in_specs=in_specs, out_specs=out_specs, check_vma=False)
```

```python
import math

import jax
import jax.numpy as jnp
from jax import lax
from jax.sharding import Mesh
from jax.sharding import PartitionSpec as P

HOT = 2
EP = ("eph", "c")


def gather_dp(x, dp_count):
    stacked = jnp.broadcast_to(x[None], (dp_count,) + x.shape)
    return lax.all_to_all(stacked, "dp", split_axis=0, concat_axis=0, tiled=True)


def silu_product(gate_part, up_part):
    return (jax.nn.silu(gate_part) * up_part).astype(jnp.bfloat16)


def local(tokens, expert_ids, gate_probs, gate_weight, up_weight, down_weight):
    pair_count = lax.axis_size("eph")
    ep_count = pair_count * HOT
    dp_count = lax.axis_size("dp")
    parity = lax.axis_index("c")
    ep_index = lax.axis_index("eph") * HOT + parity
    tok_rows, top_count = expert_ids.shape
    exp_dev = gate_weight.shape[0]
    expert_count = exp_dev * ep_count
    hot_load = min(tok_rows * 3 // 4, 4 * tok_rows * top_count // expert_count)
    cold_total = tok_rows * top_count - HOT * hot_load
    capacity = (cold_total + expert_count - HOT - 1) // (expert_count - HOT)
    host_count = pair_count
    spare_slots = max(1, math.ceil(hot_load / host_count))
    primary_slots = exp_dev * capacity

    flat_ids = expert_ids.reshape(-1)
    expert_range = jnp.arange(expert_count, dtype=jnp.int32)
    matches = (flat_ids[:, None] == expert_range[None, :]).astype(jnp.int32)
    expert_loads = jnp.sum(matches, axis=0)
    _, hot_ids = lax.top_k(expert_loads * expert_count + (expert_count - 1 - expert_range), HOT)

    own = (gate_weight[0], up_weight[0], down_weight[0])
    swapped = tuple(lax.ppermute(w, "c", [(0, 1), (1, 0)]) for w in own)
    mine = hot_ids[parity]
    my_expert = ep_index
    sibling_expert = ep_index ^ 1
    take_own = mine == my_expert
    take_sib = mine == sibling_expert
    contrib = tuple(
        jnp.where(take_own, a, jnp.where(take_sib, b, jnp.zeros_like(a)))
        for a, b in zip(own, swapped)
    )
    spare_gate, spare_up, spare_down = (lax.psum(w, "eph") for w in contrib)
    tokens, contrib = lax.optimization_barrier((tokens, contrib))

    earlier = jnp.cumsum(matches, axis=0) - matches
    order_rank = jnp.sum(earlier * matches, axis=1)
    hot_match = (flat_ids[:, None] == hot_ids[None, :]).astype(jnp.int32)
    is_hot = jnp.sum(hot_match, axis=1) > 0
    which_hot = jnp.sum(hot_match * jnp.arange(HOT, dtype=jnp.int32)[None, :], axis=1)
    spread = (ep_index * hot_load + order_rank) % host_count
    hot_target = (spread * HOT + which_hot) * spare_slots + order_rank // host_count
    cold_target = (
        flat_ids // exp_dev * primary_slots + flat_ids % exp_dev * capacity + order_rank
    )
    pick_row = jnp.arange(tok_rows * top_count, dtype=jnp.int32) // top_count
    primary_total = ep_count * primary_slots
    spare_total = ep_count * spare_slots
    cold_source = jnp.full((primary_total,), tok_rows, jnp.int32)
    cold_source = cold_source.at[jnp.where(is_hot, primary_total, cold_target)].set(
        pick_row, mode="drop"
    )
    hot_source = jnp.full((spare_total,), tok_rows, jnp.int32)
    hot_source = hot_source.at[jnp.where(is_hot, hot_target, spare_total)].set(
        pick_row, mode="drop"
    )

    feature_parts = gather_dp(tokens, dp_count)
    features = jnp.moveaxis(feature_parts, 0, 1).reshape(tok_rows, -1)
    model_width = features.shape[1]
    source_row = jnp.concatenate(
        [cold_source.reshape(ep_count, primary_slots), hot_source.reshape(ep_count, spare_slots)],
        axis=1,
    )
    outgoing = jnp.take(features, source_row, axis=0, mode="fill", fill_value=0)
    incoming = lax.all_to_all(outgoing, EP, split_axis=0, concat_axis=0, tiled=True)
    primary_rows = incoming[:, :primary_slots].reshape(ep_count, exp_dev, capacity, model_width)
    spare_rows = incoming[:, primary_slots:]

    gate_primary = jnp.einsum(
        "secd,edf->secf", primary_rows, gate_weight, preferred_element_type=jnp.float32
    )
    up_primary = jnp.einsum(
        "secd,edf->secf", primary_rows, up_weight, preferred_element_type=jnp.float32
    )
    hidden_primary = silu_product(gate_primary, up_primary)
    part_primary = gather_dp(hidden_primary, dp_count)
    feature_local = down_weight.shape[2]
    down_split = down_weight.reshape(exp_dev, dp_count, -1, feature_local)
    out_primary = jnp.einsum(
        "nsecf,enfd->secd", part_primary, down_split, preferred_element_type=jnp.float32
    ).astype(jnp.bfloat16)
    back_primary = lax.all_to_all(
        out_primary.reshape(ep_count, primary_slots, feature_local),
        EP,
        split_axis=0,
        concat_axis=0,
        tiled=True,
    ).reshape(primary_total, feature_local)

    back_primary, spare_gate, spare_up, spare_down = lax.optimization_barrier(
        (back_primary, spare_gate, spare_up, spare_down)
    )
    gate_spare = jnp.einsum(
        "srd,df->srf", spare_rows, spare_gate, preferred_element_type=jnp.float32
    )
    up_spare = jnp.einsum("srd,df->srf", spare_rows, spare_up, preferred_element_type=jnp.float32)
    hidden_spare = silu_product(gate_spare, up_spare)
    part_spare = gather_dp(hidden_spare, dp_count)
    spare_split = spare_down.reshape(dp_count, -1, feature_local)
    out_spare = jnp.einsum(
        "nsrf,nfd->srd", part_spare, spare_split, preferred_element_type=jnp.float32
    ).astype(jnp.bfloat16)
    back_spare = lax.all_to_all(out_spare, EP, split_axis=0, concat_axis=0, tiled=True).reshape(
        spare_total, feature_local
    )

    returned = jnp.concatenate([back_primary, back_spare], axis=0)
    target = jnp.where(is_hot, primary_total + hot_target, cold_target)
    fetched = jnp.take(returned, target, axis=0).reshape(tok_rows, top_count, feature_local)
    combined = jnp.sum(gate_probs[:, :, None] * fetched.astype(jnp.float32), axis=1)
    return combined.astype(jnp.bfloat16)


def solution(mesh):
    ep_size, dp_size = mesh.devices.shape
    split = Mesh(mesh.devices.reshape(ep_size // HOT, HOT, dp_size), ("eph", "c", "dp"))
    in_specs = (
        P(EP, "dp"),
        P(EP, None),
        P(EP, None),
        P(EP, None, "dp"),
        P(EP, None, "dp"),
        P(EP, None, "dp"),
    )
    out_specs = P(EP, "dp")
    return jax.shard_map(local, mesh=split, in_specs=in_specs, out_specs=out_specs, check_vma=False)
```

```python
import functools

import jax
import jax.numpy as jnp
from jax import lax
from jax.sharding import Mesh
from jax.sharding import PartitionSpec as P

HOT = 2
EP = ("eph", "c")


def copy_plan(mesh):
    column = mesh.devices[:, 0]
    place = {}
    for index, device in enumerate(column):
        coords = getattr(device, "coords", None)
        core = getattr(device, "core_on_chip", index % HOT)
        if coords is None:
            side = int(round((len(column) // HOT) ** 0.5))
            coords = (0, index // HOT % side, index // HOT // side)
        place[(coords[1], coords[2], core)] = index
    ys = 1 + max(key[0] for key in place)
    zs = 1 + max(key[1] for key in place)

    def at(y, z, c):
        return place[(y % ys, z % zs, c)]

    anchors, hosts, round_one, round_two = [], [], [[] for _ in range(5)], [[], []]
    for y0, z0 in ((0, 0), (ys // 2, zs // 2)):
        a = at(y0, z0, 0)
        first = [at(y0, z0, 1), at(y0 + 1, z0, 0), at(y0 - 1, z0, 0), at(y0, z0 + 1, 0), at(y0, z0 - 1, 0)]
        for k, dst in enumerate(first):
            round_one[k].append((a, dst))
        sib, yp, ym, zp, zm = first
        second_a = [
            (yp, at(y0 + 1, z0, 1)), (ym, at(y0 - 1, z0, 1)), (zp, at(y0, z0 + 1, 1)),
            (zm, at(y0, z0 - 1, 1)), (a, at(y0, z0 + 2, 0)), (sib, at(y0, z0 - 2, 1)),
        ]
        second_b = [
            (yp, at(y0 + 2, z0, 0)), (ym, at(y0 - 2, z0, 0)), (zp, at(y0 + 1, z0 + 1, 0)),
            (zm, at(y0 - 1, z0 - 1, 0)),
        ]
        round_two[0].extend(second_a)
        round_two[1].extend(second_b)
        anchors.append(a)
        hosts.append([a] + first + [d for _, d in second_a] + [d for _, d in second_b])
    return anchors, hosts, round_one, round_two


def gather_dp(x, dp_count):
    stacked = jnp.broadcast_to(x[None], (dp_count,) + x.shape)
    return lax.all_to_all(stacked, "dp", split_axis=0, concat_axis=0, tiled=True)


def silu_product(gate_part, up_part):
    return (jax.nn.silu(gate_part) * up_part).astype(jnp.bfloat16)


def local(plan, tokens, expert_ids, gate_probs, gate_weight, up_weight, down_weight):
    pair_count = lax.axis_size("eph")
    ep_count = pair_count * HOT
    dp_count = lax.axis_size("dp")
    parity = lax.axis_index("c")
    ep_index = lax.axis_index("eph") * HOT + parity
    tok_rows, top_count = expert_ids.shape
    exp_dev = gate_weight.shape[0]
    expert_count = exp_dev * ep_count
    hot_load = min(tok_rows * 3 // 4, 4 * tok_rows * top_count // expert_count)
    cold_total = tok_rows * top_count - HOT * hot_load
    capacity = (cold_total + expert_count - HOT - 1) // (expert_count - HOT)
    spare_slots = 1
    model_rows = gate_weight.shape[1]
    primary_slots = exp_dev * capacity

    flat_ids = expert_ids.reshape(-1)
    expert_range = jnp.arange(expert_count, dtype=jnp.int32)
    matches = (flat_ids[:, None] == expert_range[None, :]).astype(jnp.int32)
    expert_loads = jnp.sum(matches, axis=0)
    _, hot_ids = lax.top_k(expert_loads * expert_count + (expert_count - 1 - expert_range), HOT)

    anchors, hosts, round_one, round_two = plan
    assert len(hosts[0]) == hot_load
    own = jnp.concatenate(
        [gate_weight[0], up_weight[0], down_weight[0].reshape(-1, gate_weight.shape[2])], axis=0
    )
    held = jnp.zeros_like(own)
    for position in range(HOT):
        anchor = anchors[position]

        def move(w, source, anchor=anchor):
            if source == anchor:
                return w
            return lax.ppermute(w, EP, [(source, anchor)])

        branches = [lambda w, source=source: move(w, source) for source in range(ep_count)]
        moved = lax.switch(hot_ids[position], branches, own)
        held = jnp.where(ep_index == anchor, moved, held)
    tokens, held = lax.optimization_barrier((tokens, held))
    for stage in (round_one, round_two):
        received = [lax.ppermute(held, EP, pairs) for pairs in stage]
        for pairs, value in zip(stage, received):
            takers = jnp.array([d for _, d in pairs], jnp.int32)
            held = jnp.where(jnp.any(takers == ep_index), value, held)
    spare_gate = held[:model_rows]
    spare_up = held[model_rows : 2 * model_rows]
    spare_down = held[2 * model_rows :].reshape(down_weight.shape[1], down_weight.shape[2])
    host_table = jnp.array(hosts, jnp.int32)

    earlier = jnp.cumsum(matches, axis=0) - matches
    order_rank = jnp.sum(earlier * matches, axis=1)
    hot_match = (flat_ids[:, None] == hot_ids[None, :]).astype(jnp.int32)
    is_hot = jnp.sum(hot_match, axis=1) > 0
    which_hot = jnp.sum(hot_match * jnp.arange(HOT, dtype=jnp.int32)[None, :], axis=1)
    hot_target = host_table[which_hot, order_rank] * spare_slots
    cold_target = (
        flat_ids // exp_dev * primary_slots + flat_ids % exp_dev * capacity + order_rank
    )
    pick_row = jnp.arange(tok_rows * top_count, dtype=jnp.int32) // top_count
    primary_total = ep_count * primary_slots
    spare_total = ep_count * spare_slots
    cold_source = jnp.full((primary_total,), tok_rows, jnp.int32)
    cold_source = cold_source.at[jnp.where(is_hot, primary_total, cold_target)].set(
        pick_row, mode="drop"
    )
    hot_source = jnp.full((spare_total,), tok_rows, jnp.int32)
    hot_source = hot_source.at[jnp.where(is_hot, hot_target, spare_total)].set(
        pick_row, mode="drop"
    )

    feature_parts = gather_dp(tokens, dp_count)
    features = jnp.moveaxis(feature_parts, 0, 1).reshape(tok_rows, -1)
    model_width = features.shape[1]
    source_row = jnp.concatenate(
        [cold_source.reshape(ep_count, primary_slots), hot_source.reshape(ep_count, spare_slots)],
        axis=1,
    )
    outgoing = jnp.take(features, source_row, axis=0, mode="fill", fill_value=0)
    incoming = lax.all_to_all(outgoing, EP, split_axis=0, concat_axis=0, tiled=True)
    primary_rows = incoming[:, :primary_slots].reshape(ep_count, exp_dev, capacity, model_width)
    spare_rows = incoming[:, primary_slots:]

    gate_primary = jnp.einsum(
        "secd,edf->secf", primary_rows, gate_weight, preferred_element_type=jnp.float32
    )
    up_primary = jnp.einsum(
        "secd,edf->secf", primary_rows, up_weight, preferred_element_type=jnp.float32
    )
    hidden_primary = silu_product(gate_primary, up_primary)
    part_primary = gather_dp(hidden_primary, dp_count)
    feature_local = down_weight.shape[2]
    down_split = down_weight.reshape(exp_dev, dp_count, -1, feature_local)
    out_primary = jnp.einsum(
        "nsecf,enfd->secd", part_primary, down_split, preferred_element_type=jnp.float32
    ).astype(jnp.bfloat16)
    back_primary = lax.all_to_all(
        out_primary.reshape(ep_count, primary_slots, feature_local),
        EP,
        split_axis=0,
        concat_axis=0,
        tiled=True,
    ).reshape(primary_total, feature_local)

    back_primary, spare_gate, spare_up, spare_down = lax.optimization_barrier(
        (back_primary, spare_gate, spare_up, spare_down)
    )
    gate_spare = jnp.einsum(
        "srd,df->srf", spare_rows, spare_gate, preferred_element_type=jnp.float32
    )
    up_spare = jnp.einsum("srd,df->srf", spare_rows, spare_up, preferred_element_type=jnp.float32)
    hidden_spare = silu_product(gate_spare, up_spare)
    part_spare = gather_dp(hidden_spare, dp_count)
    spare_split = spare_down.reshape(dp_count, -1, feature_local)
    out_spare = jnp.einsum(
        "nsrf,nfd->srd", part_spare, spare_split, preferred_element_type=jnp.float32
    ).astype(jnp.bfloat16)
    back_spare = lax.all_to_all(out_spare, EP, split_axis=0, concat_axis=0, tiled=True).reshape(
        spare_total, feature_local
    )

    returned = jnp.concatenate([back_primary, back_spare], axis=0)
    target = jnp.where(is_hot, primary_total + hot_target, cold_target)
    fetched = jnp.take(returned, target, axis=0).reshape(tok_rows, top_count, feature_local)
    combined = jnp.sum(gate_probs[:, :, None] * fetched.astype(jnp.float32), axis=1)
    return combined.astype(jnp.bfloat16)


def solution(mesh):
    ep_size, dp_size = mesh.devices.shape
    split = Mesh(mesh.devices.reshape(ep_size // HOT, HOT, dp_size), ("eph", "c", "dp"))
    in_specs = (
        P(EP, "dp"),
        P(EP, None),
        P(EP, None),
        P(EP, None, "dp"),
        P(EP, None, "dp"),
        P(EP, None, "dp"),
    )
    out_specs = P(EP, "dp")
    plan = copy_plan(mesh)
    return jax.shard_map(functools.partial(local, plan), mesh=split, in_specs=in_specs, out_specs=out_specs, check_vma=False)
```

```python
import math

import jax
import jax.numpy as jnp
from jax import lax
from jax.sharding import Mesh
from jax.sharding import PartitionSpec as P

HOT = 2
EP = ("eph", "c")


def gather_dp(x, dp_count):
    stacked = jnp.broadcast_to(x[None], (dp_count,) + x.shape)
    return lax.all_to_all(stacked, "dp", split_axis=0, concat_axis=0, tiled=True)


def silu_product(gate_part, up_part):
    return (jax.nn.silu(gate_part) * up_part).astype(jnp.bfloat16)


def local(tokens, expert_ids, gate_probs, gate_weight, up_weight, down_weight):
    pair_count = lax.axis_size("eph")
    ep_count = pair_count * HOT
    dp_count = lax.axis_size("dp")
    parity = lax.axis_index("c")
    ep_index = lax.axis_index("eph") * HOT + parity
    tok_rows, top_count = expert_ids.shape
    exp_dev = gate_weight.shape[0]
    expert_count = exp_dev * ep_count
    hot_load = min(tok_rows * 3 // 4, 4 * tok_rows * top_count // expert_count)
    cold_total = tok_rows * top_count - HOT * hot_load
    capacity = (cold_total + expert_count - HOT - 1) // (expert_count - HOT)
    host_count = pair_count
    spare_slots = max(1, math.ceil(hot_load / host_count))
    primary_slots = exp_dev * capacity

    flat_ids = expert_ids.reshape(-1)
    expert_range = jnp.arange(expert_count, dtype=jnp.int32)
    matches = (flat_ids[:, None] == expert_range[None, :]).astype(jnp.int32)
    expert_loads = jnp.sum(matches, axis=0)
    _, hot_ids = lax.top_k(expert_loads * expert_count + (expert_count - 1 - expert_range), HOT)

    own = (gate_weight[0], up_weight[0], down_weight[0])
    swapped = tuple(lax.ppermute(w, "c", [(0, 1), (1, 0)]) for w in own)
    mine = hot_ids[parity]
    my_expert = ep_index
    sibling_expert = ep_index ^ 1
    take_own = mine == my_expert
    take_sib = mine == sibling_expert
    contrib = tuple(
        jnp.where(take_own, a, jnp.where(take_sib, b, jnp.zeros_like(a)))
        for a, b in zip(own, swapped)
    )
    packed = jnp.concatenate(
        [contrib[0], contrib[1], contrib[2].reshape(-1, contrib[0].shape[1])], axis=0
    )
    piece = lax.psum_scatter(packed, "eph", scatter_dimension=0, tiled=True)
    spread_back = lax.all_gather(piece, "eph", axis=0, tiled=True)
    model_rows = contrib[0].shape[0]
    spare_gate = spread_back[:model_rows]
    spare_up = spread_back[model_rows : 2 * model_rows]
    spare_down = spread_back[2 * model_rows :].reshape(contrib[2].shape)
    tokens, contrib = lax.optimization_barrier((tokens, contrib))

    earlier = jnp.cumsum(matches, axis=0) - matches
    order_rank = jnp.sum(earlier * matches, axis=1)
    hot_match = (flat_ids[:, None] == hot_ids[None, :]).astype(jnp.int32)
    is_hot = jnp.sum(hot_match, axis=1) > 0
    which_hot = jnp.sum(hot_match * jnp.arange(HOT, dtype=jnp.int32)[None, :], axis=1)
    spread = (ep_index * hot_load + order_rank) % host_count
    hot_target = (spread * HOT + which_hot) * spare_slots + order_rank // host_count
    cold_target = (
        flat_ids // exp_dev * primary_slots + flat_ids % exp_dev * capacity + order_rank
    )
    pick_row = jnp.arange(tok_rows * top_count, dtype=jnp.int32) // top_count
    primary_total = ep_count * primary_slots
    spare_total = ep_count * spare_slots
    cold_source = jnp.full((primary_total,), tok_rows, jnp.int32)
    cold_source = cold_source.at[jnp.where(is_hot, primary_total, cold_target)].set(
        pick_row, mode="drop"
    )
    hot_source = jnp.full((spare_total,), tok_rows, jnp.int32)
    hot_source = hot_source.at[jnp.where(is_hot, hot_target, spare_total)].set(
        pick_row, mode="drop"
    )

    feature_parts = gather_dp(tokens, dp_count)
    features = jnp.moveaxis(feature_parts, 0, 1).reshape(tok_rows, -1)
    model_width = features.shape[1]
    source_row = jnp.concatenate(
        [cold_source.reshape(ep_count, primary_slots), hot_source.reshape(ep_count, spare_slots)],
        axis=1,
    )
    outgoing = jnp.take(features, source_row, axis=0, mode="fill", fill_value=0)
    incoming = lax.all_to_all(outgoing, EP, split_axis=0, concat_axis=0, tiled=True)
    primary_rows = incoming[:, :primary_slots].reshape(ep_count, exp_dev, capacity, model_width)
    spare_rows = incoming[:, primary_slots:]

    gate_primary = jnp.einsum(
        "secd,edf->secf", primary_rows, gate_weight, preferred_element_type=jnp.float32
    )
    up_primary = jnp.einsum(
        "secd,edf->secf", primary_rows, up_weight, preferred_element_type=jnp.float32
    )
    hidden_primary = silu_product(gate_primary, up_primary)
    part_primary = gather_dp(hidden_primary, dp_count)
    feature_local = down_weight.shape[2]
    down_split = down_weight.reshape(exp_dev, dp_count, -1, feature_local)
    out_primary = jnp.einsum(
        "nsecf,enfd->secd", part_primary, down_split, preferred_element_type=jnp.float32
    ).astype(jnp.bfloat16)
    back_primary = lax.all_to_all(
        out_primary.reshape(ep_count, primary_slots, feature_local),
        EP,
        split_axis=0,
        concat_axis=0,
        tiled=True,
    ).reshape(primary_total, feature_local)

    back_primary, spare_gate, spare_up, spare_down = lax.optimization_barrier(
        (back_primary, spare_gate, spare_up, spare_down)
    )
    gate_spare = jnp.einsum(
        "srd,df->srf", spare_rows, spare_gate, preferred_element_type=jnp.float32
    )
    up_spare = jnp.einsum("srd,df->srf", spare_rows, spare_up, preferred_element_type=jnp.float32)
    hidden_spare = silu_product(gate_spare, up_spare)
    part_spare = gather_dp(hidden_spare, dp_count)
    spare_split = spare_down.reshape(dp_count, -1, feature_local)
    out_spare = jnp.einsum(
        "nsrf,nfd->srd", part_spare, spare_split, preferred_element_type=jnp.float32
    ).astype(jnp.bfloat16)
    back_spare = lax.all_to_all(out_spare, EP, split_axis=0, concat_axis=0, tiled=True).reshape(
        spare_total, feature_local
    )

    returned = jnp.concatenate([back_primary, back_spare], axis=0)
    target = jnp.where(is_hot, primary_total + hot_target, cold_target)
    fetched = jnp.take(returned, target, axis=0).reshape(tok_rows, top_count, feature_local)
    combined = jnp.sum(gate_probs[:, :, None] * fetched.astype(jnp.float32), axis=1)
    return combined.astype(jnp.bfloat16)


def solution(mesh):
    ep_size, dp_size = mesh.devices.shape
    split = Mesh(mesh.devices.reshape(ep_size // HOT, HOT, dp_size), ("eph", "c", "dp"))
    in_specs = (
        P(EP, "dp"),
        P(EP, None),
        P(EP, None),
        P(EP, None, "dp"),
        P(EP, None, "dp"),
        P(EP, None, "dp"),
    )
    out_specs = P(EP, "dp")
    return jax.shard_map(local, mesh=split, in_specs=in_specs, out_specs=out_specs, check_vma=False)
```

```python
import math

import jax
import jax.numpy as jnp
from jax import lax
from jax.sharding import Mesh
from jax.sharding import PartitionSpec as P

HOT = 2
EP = ("eph", "c")


def gather_dp(x, dp_count):
    stacked = jnp.broadcast_to(x[None], (dp_count,) + x.shape)
    return lax.all_to_all(stacked, "dp", split_axis=0, concat_axis=0, tiled=True)


def silu_product(gate_part, up_part):
    return (jax.nn.silu(gate_part) * up_part).astype(jnp.bfloat16)


def local(tokens, expert_ids, gate_probs, gate_weight, up_weight, down_weight):
    pair_count = lax.axis_size("eph")
    ep_count = pair_count * HOT
    dp_count = lax.axis_size("dp")
    parity = lax.axis_index("c")
    ep_index = lax.axis_index("eph") * HOT + parity
    tok_rows, top_count = expert_ids.shape
    exp_dev = gate_weight.shape[0]
    expert_count = exp_dev * ep_count
    hot_load = min(tok_rows * 3 // 4, 4 * tok_rows * top_count // expert_count)
    cold_total = tok_rows * top_count - HOT * hot_load
    capacity = (cold_total + expert_count - HOT - 1) // (expert_count - HOT)
    host_count = pair_count
    spare_slots = max(1, math.ceil(hot_load / host_count))
    primary_slots = exp_dev * capacity

    flat_ids = expert_ids.reshape(-1)
    expert_range = jnp.arange(expert_count, dtype=jnp.int32)
    matches = (flat_ids[:, None] == expert_range[None, :]).astype(jnp.int32)
    expert_loads = jnp.sum(matches, axis=0)
    _, hot_ids = lax.top_k(expert_loads * expert_count + (expert_count - 1 - expert_range), HOT)

    own = (gate_weight[0], up_weight[0], down_weight[0])
    swapped = tuple(lax.ppermute(w, "c", [(0, 1), (1, 0)]) for w in own)
    mine = hot_ids[parity]
    my_expert = ep_index
    sibling_expert = ep_index ^ 1
    take_own = mine == my_expert
    take_sib = mine == sibling_expert
    contrib = tuple(
        jnp.where(take_own, a, jnp.where(take_sib, b, jnp.zeros_like(a)))
        for a, b in zip(own, swapped)
    )
    packed = jnp.concatenate(
        [contrib[0], contrib[1], contrib[2].reshape(-1, contrib[0].shape[1])], axis=0
    )
    blocks = packed.reshape(pair_count, -1, packed.shape[1])
    pieces = lax.all_to_all(blocks, "eph", split_axis=0, concat_axis=0, tiled=True)
    piece = lax.dynamic_index_in_dim(pieces, hot_ids[parity] // HOT, axis=0, keepdims=False)
    spread_back = lax.all_gather(piece, "eph", axis=0, tiled=True)
    model_rows = contrib[0].shape[0]
    spare_gate = spread_back[:model_rows]
    spare_up = spread_back[model_rows : 2 * model_rows]
    spare_down = spread_back[2 * model_rows :].reshape(contrib[2].shape)
    tokens, contrib = lax.optimization_barrier((tokens, contrib))

    earlier = jnp.cumsum(matches, axis=0) - matches
    order_rank = jnp.sum(earlier * matches, axis=1)
    hot_match = (flat_ids[:, None] == hot_ids[None, :]).astype(jnp.int32)
    is_hot = jnp.sum(hot_match, axis=1) > 0
    which_hot = jnp.sum(hot_match * jnp.arange(HOT, dtype=jnp.int32)[None, :], axis=1)
    spread = (ep_index * hot_load + order_rank) % host_count
    hot_target = (spread * HOT + which_hot) * spare_slots + order_rank // host_count
    cold_target = (
        flat_ids // exp_dev * primary_slots + flat_ids % exp_dev * capacity + order_rank
    )
    pick_row = jnp.arange(tok_rows * top_count, dtype=jnp.int32) // top_count
    primary_total = ep_count * primary_slots
    spare_total = ep_count * spare_slots
    cold_source = jnp.full((primary_total,), tok_rows, jnp.int32)
    cold_source = cold_source.at[jnp.where(is_hot, primary_total, cold_target)].set(
        pick_row, mode="drop"
    )
    hot_source = jnp.full((spare_total,), tok_rows, jnp.int32)
    hot_source = hot_source.at[jnp.where(is_hot, hot_target, spare_total)].set(
        pick_row, mode="drop"
    )

    feature_parts = gather_dp(tokens, dp_count)
    features = jnp.moveaxis(feature_parts, 0, 1).reshape(tok_rows, -1)
    model_width = features.shape[1]
    source_row = jnp.concatenate(
        [cold_source.reshape(ep_count, primary_slots), hot_source.reshape(ep_count, spare_slots)],
        axis=1,
    )
    outgoing = jnp.take(features, source_row, axis=0, mode="fill", fill_value=0)
    incoming = lax.all_to_all(outgoing, EP, split_axis=0, concat_axis=0, tiled=True)
    primary_rows = incoming[:, :primary_slots].reshape(ep_count, exp_dev, capacity, model_width)
    spare_rows = incoming[:, primary_slots:]

    gate_primary = jnp.einsum(
        "secd,edf->secf", primary_rows, gate_weight, preferred_element_type=jnp.float32
    )
    up_primary = jnp.einsum(
        "secd,edf->secf", primary_rows, up_weight, preferred_element_type=jnp.float32
    )
    hidden_primary = silu_product(gate_primary, up_primary)
    part_primary = gather_dp(hidden_primary, dp_count)
    feature_local = down_weight.shape[2]
    down_split = down_weight.reshape(exp_dev, dp_count, -1, feature_local)
    out_primary = jnp.einsum(
        "nsecf,enfd->secd", part_primary, down_split, preferred_element_type=jnp.float32
    ).astype(jnp.bfloat16)
    back_primary = lax.all_to_all(
        out_primary.reshape(ep_count, primary_slots, feature_local),
        EP,
        split_axis=0,
        concat_axis=0,
        tiled=True,
    ).reshape(primary_total, feature_local)

    back_primary, spare_gate, spare_up, spare_down = lax.optimization_barrier(
        (back_primary, spare_gate, spare_up, spare_down)
    )
    gate_spare = jnp.einsum(
        "srd,df->srf", spare_rows, spare_gate, preferred_element_type=jnp.float32
    )
    up_spare = jnp.einsum("srd,df->srf", spare_rows, spare_up, preferred_element_type=jnp.float32)
    hidden_spare = silu_product(gate_spare, up_spare)
    part_spare = gather_dp(hidden_spare, dp_count)
    spare_split = spare_down.reshape(dp_count, -1, feature_local)
    out_spare = jnp.einsum(
        "nsrf,nfd->srd", part_spare, spare_split, preferred_element_type=jnp.float32
    ).astype(jnp.bfloat16)
    back_spare = lax.all_to_all(out_spare, EP, split_axis=0, concat_axis=0, tiled=True).reshape(
        spare_total, feature_local
    )

    returned = jnp.concatenate([back_primary, back_spare], axis=0)
    target = jnp.where(is_hot, primary_total + hot_target, cold_target)
    fetched = jnp.take(returned, target, axis=0).reshape(tok_rows, top_count, feature_local)
    combined = jnp.sum(gate_probs[:, :, None] * fetched.astype(jnp.float32), axis=1)
    return combined.astype(jnp.bfloat16)


def solution(mesh):
    ep_size, dp_size = mesh.devices.shape
    split = Mesh(mesh.devices.reshape(ep_size // HOT, HOT, dp_size), ("eph", "c", "dp"))
    in_specs = (
        P(EP, "dp"),
        P(EP, None),
        P(EP, None),
        P(EP, None, "dp"),
        P(EP, None, "dp"),
        P(EP, None, "dp"),
    )
    out_specs = P(EP, "dp")
    return jax.shard_map(local, mesh=split, in_specs=in_specs, out_specs=out_specs, check_vma=False)
```

```python
import math

import jax
import jax.numpy as jnp
from jax import lax
from jax.sharding import Mesh
from jax.sharding import PartitionSpec as P

HOT = 2
EP = ("eph", "c")


def gather_dp(x, dp_count):
    stacked = jnp.broadcast_to(x[None], (dp_count,) + x.shape)
    return lax.all_to_all(stacked, "dp", split_axis=0, concat_axis=0, tiled=True)


def silu_product(gate_part, up_part):
    return (jax.nn.silu(gate_part) * up_part).astype(jnp.bfloat16)


def local(tokens, expert_ids, gate_probs, gate_weight, up_weight, down_weight):
    pair_count = lax.axis_size("eph")
    ep_count = pair_count * HOT
    dp_count = lax.axis_size("dp")
    parity = lax.axis_index("c")
    ep_index = lax.axis_index("eph") * HOT + parity
    tok_rows, top_count = expert_ids.shape
    exp_dev = gate_weight.shape[0]
    expert_count = exp_dev * ep_count
    hot_load = min(tok_rows * 3 // 4, 4 * tok_rows * top_count // expert_count)
    cold_total = tok_rows * top_count - HOT * hot_load
    capacity = (cold_total + expert_count - HOT - 1) // (expert_count - HOT)
    host_count = pair_count
    spare_slots = max(1, math.ceil(hot_load / host_count))
    primary_slots = exp_dev * capacity

    flat_ids = expert_ids.reshape(-1)
    expert_range = jnp.arange(expert_count, dtype=jnp.int32)
    matches = (flat_ids[:, None] == expert_range[None, :]).astype(jnp.int32)
    expert_loads = jnp.sum(matches, axis=0)
    _, hot_ids = lax.top_k(expert_loads * expert_count + (expert_count - 1 - expert_range), HOT)

    own = (gate_weight[0], up_weight[0], down_weight[0])
    swapped = tuple(lax.ppermute(w, "c", [(0, 1), (1, 0)]) for w in own)
    mine = hot_ids[parity]
    my_expert = ep_index
    sibling_expert = ep_index ^ 1
    take_own = mine == my_expert
    take_sib = mine == sibling_expert
    contrib = tuple(
        jnp.where(take_own, a, jnp.where(take_sib, b, jnp.zeros_like(a)))
        for a, b in zip(own, swapped)
    )
    packed = jnp.concatenate(
        [contrib[0], contrib[1], contrib[2].reshape(-1, contrib[0].shape[1])], axis=0
    )
    blocks = packed.reshape(pair_count, -1, packed.shape[1])
    pieces = lax.all_to_all(blocks, "eph", split_axis=0, concat_axis=0, tiled=True)
    piece = lax.dynamic_index_in_dim(pieces, hot_ids[parity] // HOT, axis=0, keepdims=False)
    spread_back = lax.all_gather(piece, "eph", axis=0, tiled=True)
    model_rows = contrib[0].shape[0]
    spare_gate = spread_back[:model_rows]
    spare_up = spread_back[model_rows : 2 * model_rows]
    spare_down = spread_back[2 * model_rows :].reshape(contrib[2].shape)
    tokens, contrib = lax.optimization_barrier((tokens, contrib))

    earlier = jnp.cumsum(matches, axis=0) - matches
    order_rank = jnp.sum(earlier * matches, axis=1)
    hot_match = (flat_ids[:, None] == hot_ids[None, :]).astype(jnp.int32)
    is_hot = jnp.sum(hot_match, axis=1) > 0
    which_hot = jnp.sum(hot_match * jnp.arange(HOT, dtype=jnp.int32)[None, :], axis=1)
    spread = (ep_index * hot_load + order_rank) % host_count
    hot_target = (spread * HOT + which_hot) * spare_slots + order_rank // host_count
    cold_target = (
        flat_ids // exp_dev * primary_slots + flat_ids % exp_dev * capacity + order_rank
    )
    pick_row = jnp.arange(tok_rows * top_count, dtype=jnp.int32) // top_count
    primary_total = ep_count * primary_slots
    spare_total = ep_count * spare_slots
    cold_source = jnp.full((primary_total,), tok_rows, jnp.int32)
    cold_source = cold_source.at[jnp.where(is_hot, primary_total, cold_target)].set(
        pick_row, mode="drop"
    )
    hot_source = jnp.full((spare_total,), tok_rows, jnp.int32)
    hot_source = hot_source.at[jnp.where(is_hot, hot_target, spare_total)].set(
        pick_row, mode="drop"
    )

    slice_width = tokens.shape[1]
    source_row = jnp.concatenate(
        [cold_source.reshape(ep_count, primary_slots), hot_source.reshape(ep_count, spare_slots)],
        axis=1,
    )
    outgoing = jnp.take(tokens, source_row, axis=0, mode="fill", fill_value=0)
    arrived = lax.all_to_all(outgoing, EP, split_axis=0, concat_axis=0, tiled=True)
    incoming = gather_dp(arrived, dp_count)
    primary_rows = incoming[:, :, :primary_slots].reshape(
        dp_count, ep_count, exp_dev, capacity, slice_width
    )
    spare_rows = incoming[:, :, primary_slots:]
    gate_split = gate_weight.reshape(exp_dev, dp_count, slice_width, -1)
    up_split = up_weight.reshape(exp_dev, dp_count, slice_width, -1)

    gate_primary = jnp.einsum(
        "nsecd,endf->secf", primary_rows, gate_split, preferred_element_type=jnp.float32
    )
    up_primary = jnp.einsum(
        "nsecd,endf->secf", primary_rows, up_split, preferred_element_type=jnp.float32
    )
    hidden_primary = silu_product(gate_primary, up_primary)
    part_primary = gather_dp(hidden_primary, dp_count)
    feature_local = down_weight.shape[2]
    down_split = down_weight.reshape(exp_dev, dp_count, -1, feature_local)
    out_primary = jnp.einsum(
        "nsecf,enfd->secd", part_primary, down_split, preferred_element_type=jnp.float32
    ).astype(jnp.bfloat16)
    back_primary = lax.all_to_all(
        out_primary.reshape(ep_count, primary_slots, feature_local),
        EP,
        split_axis=0,
        concat_axis=0,
        tiled=True,
    ).reshape(primary_total, feature_local)

    back_primary, spare_gate, spare_up, spare_down = lax.optimization_barrier(
        (back_primary, spare_gate, spare_up, spare_down)
    )
    spare_gate = spare_gate.reshape(dp_count, slice_width, -1)
    spare_up = spare_up.reshape(dp_count, slice_width, -1)
    gate_spare = jnp.einsum(
        "nsrd,ndf->srf", spare_rows, spare_gate, preferred_element_type=jnp.float32
    )
    up_spare = jnp.einsum(
        "nsrd,ndf->srf", spare_rows, spare_up, preferred_element_type=jnp.float32
    )
    hidden_spare = silu_product(gate_spare, up_spare)
    part_spare = gather_dp(hidden_spare, dp_count)
    spare_split = spare_down.reshape(dp_count, -1, feature_local)
    out_spare = jnp.einsum(
        "nsrf,nfd->srd", part_spare, spare_split, preferred_element_type=jnp.float32
    ).astype(jnp.bfloat16)
    back_spare = lax.all_to_all(out_spare, EP, split_axis=0, concat_axis=0, tiled=True).reshape(
        spare_total, feature_local
    )

    returned = jnp.concatenate([back_primary, back_spare], axis=0)
    target = jnp.where(is_hot, primary_total + hot_target, cold_target)
    fetched = jnp.take(returned, target, axis=0).reshape(tok_rows, top_count, feature_local)
    combined = jnp.sum(gate_probs[:, :, None] * fetched.astype(jnp.float32), axis=1)
    return combined.astype(jnp.bfloat16)


def solution(mesh):
    ep_size, dp_size = mesh.devices.shape
    split = Mesh(mesh.devices.reshape(ep_size // HOT, HOT, dp_size), ("eph", "c", "dp"))
    in_specs = (
        P(EP, "dp"),
        P(EP, None),
        P(EP, None),
        P(EP, None, "dp"),
        P(EP, None, "dp"),
        P(EP, None, "dp"),
    )
    out_specs = P(EP, "dp")
    return jax.shard_map(local, mesh=split, in_specs=in_specs, out_specs=out_specs, check_vma=False)
```

```python
import math

import jax
import jax.numpy as jnp
from jax import lax
from jax.sharding import Mesh
from jax.sharding import PartitionSpec as P

HOT = 2
EP = ("eph", "c")


def gather_dp(x, dp_count):
    stacked = jnp.broadcast_to(x[None], (dp_count,) + x.shape)
    return lax.all_to_all(stacked, "dp", split_axis=0, concat_axis=0, tiled=True)


def silu_product(gate_part, up_part):
    return (jax.nn.silu(gate_part) * up_part).astype(jnp.bfloat16)


def local(tokens, expert_ids, gate_probs, gate_weight, up_weight, down_weight):
    pair_count = lax.axis_size("eph")
    ep_count = pair_count * HOT
    dp_count = lax.axis_size("dp")
    parity = lax.axis_index("c")
    ep_index = lax.axis_index("eph") * HOT + parity
    tok_rows, top_count = expert_ids.shape
    exp_dev = gate_weight.shape[0]
    expert_count = exp_dev * ep_count
    hot_load = min(tok_rows * 3 // 4, 4 * tok_rows * top_count // expert_count)
    cold_total = tok_rows * top_count - HOT * hot_load
    capacity = (cold_total + expert_count - HOT - 1) // (expert_count - HOT)
    host_count = pair_count
    spare_slots = max(1, math.ceil(hot_load / host_count))
    primary_slots = exp_dev * capacity

    flat_ids = expert_ids.reshape(-1)
    expert_range = jnp.arange(expert_count, dtype=jnp.int32)
    matches = (flat_ids[:, None] == expert_range[None, :]).astype(jnp.int32)
    expert_loads = jnp.sum(matches, axis=0)
    _, hot_ids = lax.top_k(expert_loads * expert_count + (expert_count - 1 - expert_range), HOT)

    own = (gate_weight[0], up_weight[0], down_weight[0])
    swapped = tuple(lax.ppermute(w, "c", [(0, 1), (1, 0)]) for w in own)
    mine = hot_ids[parity]
    my_expert = ep_index
    sibling_expert = ep_index ^ 1
    take_own = mine == my_expert
    take_sib = mine == sibling_expert
    contrib = tuple(
        jnp.where(take_own, a, jnp.where(take_sib, b, jnp.zeros_like(a)))
        for a, b in zip(own, swapped)
    )
    packed = jnp.concatenate(
        [contrib[0], contrib[1], contrib[2].reshape(-1, contrib[0].shape[1])], axis=0
    )
    blocks = packed.reshape(pair_count, -1, packed.shape[1])
    pieces = lax.all_to_all(blocks, "eph", split_axis=0, concat_axis=0, tiled=True)
    piece = lax.dynamic_index_in_dim(pieces, hot_ids[parity] // HOT, axis=0, keepdims=False)
    spread_back = lax.all_gather(piece, "eph", axis=0, tiled=True)
    model_rows = contrib[0].shape[0]
    spare_gate = spread_back[:model_rows]
    spare_up = spread_back[model_rows : 2 * model_rows]
    spare_down = spread_back[2 * model_rows :].reshape(contrib[2].shape)
    tokens, contrib = lax.optimization_barrier((tokens, contrib))

    earlier = jnp.cumsum(matches, axis=0) - matches
    order_rank = jnp.sum(earlier * matches, axis=1)
    hot_match = (flat_ids[:, None] == hot_ids[None, :]).astype(jnp.int32)
    is_hot = jnp.sum(hot_match, axis=1) > 0
    which_hot = jnp.sum(hot_match * jnp.arange(HOT, dtype=jnp.int32)[None, :], axis=1)
    spread = (ep_index * hot_load + order_rank) % host_count
    hot_target = (spread * HOT + which_hot) * spare_slots + order_rank // host_count
    cold_target = (
        flat_ids // exp_dev * primary_slots + flat_ids % exp_dev * capacity + order_rank
    )
    pick_row = jnp.arange(tok_rows * top_count, dtype=jnp.int32) // top_count
    primary_total = ep_count * primary_slots
    spare_total = ep_count * spare_slots
    cold_source = jnp.full((primary_total,), tok_rows, jnp.int32)
    cold_source = cold_source.at[jnp.where(is_hot, primary_total, cold_target)].set(
        pick_row, mode="drop"
    )
    hot_source = jnp.full((spare_total,), tok_rows, jnp.int32)
    hot_source = hot_source.at[jnp.where(is_hot, hot_target, spare_total)].set(
        pick_row, mode="drop"
    )

    slice_width = tokens.shape[1]
    source_row = jnp.concatenate(
        [cold_source.reshape(ep_count, primary_slots), hot_source.reshape(ep_count, spare_slots)],
        axis=1,
    )
    outgoing = jnp.take(tokens, source_row, axis=0, mode="fill", fill_value=0)
    arrived = lax.all_to_all(outgoing, EP, split_axis=0, concat_axis=0, tiled=True)
    incoming = gather_dp(arrived, dp_count)
    primary_rows = incoming[:, :, :primary_slots].reshape(
        dp_count, ep_count, exp_dev, capacity, slice_width
    )
    spare_rows = incoming[:, :, primary_slots:]
    gate_split = gate_weight.reshape(exp_dev, dp_count, slice_width, -1)
    up_split = up_weight.reshape(exp_dev, dp_count, slice_width, -1)

    gate_primary = jnp.einsum(
        "nsecd,endf->secf", primary_rows, gate_split, preferred_element_type=jnp.float32
    )
    up_primary = jnp.einsum(
        "nsecd,endf->secf", primary_rows, up_split, preferred_element_type=jnp.float32
    )
    hidden_primary = silu_product(gate_primary, up_primary)
    part_primary = gather_dp(hidden_primary, dp_count)
    feature_local = down_weight.shape[2]
    down_split = down_weight.reshape(exp_dev, dp_count, -1, feature_local)
    out_primary = jnp.einsum(
        "nsecf,enfd->secd", part_primary, down_split, preferred_element_type=jnp.float32
    ).astype(jnp.bfloat16)

    spare_gate = spare_gate.reshape(dp_count, slice_width, -1)
    spare_up = spare_up.reshape(dp_count, slice_width, -1)
    gate_spare = jnp.einsum(
        "nsrd,ndf->srf", spare_rows, spare_gate, preferred_element_type=jnp.float32
    )
    up_spare = jnp.einsum(
        "nsrd,ndf->srf", spare_rows, spare_up, preferred_element_type=jnp.float32
    )
    hidden_spare = silu_product(gate_spare, up_spare)
    part_spare = gather_dp(hidden_spare, dp_count)
    spare_split = spare_down.reshape(dp_count, -1, feature_local)
    out_spare = jnp.einsum(
        "nsrf,nfd->srd", part_spare, spare_split, preferred_element_type=jnp.float32
    ).astype(jnp.bfloat16)

    per_owner = primary_slots + spare_slots
    results = jnp.concatenate(
        [out_primary.reshape(ep_count, primary_slots, feature_local), out_spare], axis=1
    )
    returned = lax.all_to_all(results, EP, split_axis=0, concat_axis=0, tiled=True).reshape(
        ep_count * per_owner, feature_local
    )
    cold_back = (
        flat_ids // exp_dev * per_owner + flat_ids % exp_dev * capacity + order_rank
    )
    hot_back = (
        hot_target // spare_slots * per_owner + primary_slots + hot_target % spare_slots
    )
    target = jnp.where(is_hot, hot_back, cold_back)
    fetched = jnp.take(returned, target, axis=0).reshape(tok_rows, top_count, feature_local)
    combined = jnp.sum(gate_probs[:, :, None] * fetched.astype(jnp.float32), axis=1)
    return combined.astype(jnp.bfloat16)


def solution(mesh):
    ep_size, dp_size = mesh.devices.shape
    split = Mesh(mesh.devices.reshape(ep_size // HOT, HOT, dp_size), ("eph", "c", "dp"))
    in_specs = (
        P(EP, "dp"),
        P(EP, None),
        P(EP, None),
        P(EP, None, "dp"),
        P(EP, None, "dp"),
        P(EP, None, "dp"),
    )
    out_specs = P(EP, "dp")
    return jax.shard_map(local, mesh=split, in_specs=in_specs, out_specs=out_specs, check_vma=False)
```

```python
import math

import jax
import jax.numpy as jnp
from jax import lax
from jax.sharding import Mesh
from jax.sharding import PartitionSpec as P

HOT = 2
EP = ("eph", "c")


def gather_dp(x, dp_count):
    parts = [x] + [
        lax.ppermute(x, "dp", [(i, (i + k) % dp_count) for i in range(dp_count)])
        for k in range(1, dp_count)
    ]
    stacked = jnp.stack(parts)
    here = lax.axis_index("dp")
    order = (here - jnp.arange(dp_count, dtype=jnp.int32)) % dp_count
    return jnp.take(stacked, order, axis=0)


def silu_product(gate_part, up_part):
    return (jax.nn.silu(gate_part) * up_part).astype(jnp.bfloat16)


def local(tokens, expert_ids, gate_probs, gate_weight, up_weight, down_weight):
    pair_count = lax.axis_size("eph")
    ep_count = pair_count * HOT
    dp_count = lax.axis_size("dp")
    parity = lax.axis_index("c")
    ep_index = lax.axis_index("eph") * HOT + parity
    tok_rows, top_count = expert_ids.shape
    exp_dev = gate_weight.shape[0]
    expert_count = exp_dev * ep_count
    hot_load = min(tok_rows * 3 // 4, 4 * tok_rows * top_count // expert_count)
    cold_total = tok_rows * top_count - HOT * hot_load
    capacity = (cold_total + expert_count - HOT - 1) // (expert_count - HOT)
    host_count = pair_count
    spare_slots = max(1, math.ceil(hot_load / host_count))
    primary_slots = exp_dev * capacity

    flat_ids = expert_ids.reshape(-1)
    expert_range = jnp.arange(expert_count, dtype=jnp.int32)
    matches = (flat_ids[:, None] == expert_range[None, :]).astype(jnp.int32)
    expert_loads = jnp.sum(matches, axis=0)
    _, hot_ids = lax.top_k(expert_loads * expert_count + (expert_count - 1 - expert_range), HOT)

    own = (gate_weight[0], up_weight[0], down_weight[0])
    swapped = tuple(lax.ppermute(w, "c", [(0, 1), (1, 0)]) for w in own)
    mine = hot_ids[parity]
    my_expert = ep_index
    sibling_expert = ep_index ^ 1
    take_own = mine == my_expert
    take_sib = mine == sibling_expert
    contrib = tuple(
        jnp.where(take_own, a, jnp.where(take_sib, b, jnp.zeros_like(a)))
        for a, b in zip(own, swapped)
    )
    packed = jnp.concatenate(
        [contrib[0], contrib[1], contrib[2].reshape(-1, contrib[0].shape[1])], axis=0
    )
    blocks = packed.reshape(pair_count, -1, packed.shape[1])
    pieces = lax.all_to_all(blocks, "eph", split_axis=0, concat_axis=0, tiled=True)
    piece = lax.dynamic_index_in_dim(pieces, hot_ids[parity] // HOT, axis=0, keepdims=False)
    spread_back = lax.all_gather(piece, "eph", axis=0, tiled=True)
    model_rows = contrib[0].shape[0]
    spare_gate = spread_back[:model_rows]
    spare_up = spread_back[model_rows : 2 * model_rows]
    spare_down = spread_back[2 * model_rows :].reshape(contrib[2].shape)
    tokens, contrib = lax.optimization_barrier((tokens, contrib))

    earlier = jnp.cumsum(matches, axis=0) - matches
    order_rank = jnp.sum(earlier * matches, axis=1)
    hot_match = (flat_ids[:, None] == hot_ids[None, :]).astype(jnp.int32)
    is_hot = jnp.sum(hot_match, axis=1) > 0
    which_hot = jnp.sum(hot_match * jnp.arange(HOT, dtype=jnp.int32)[None, :], axis=1)
    spread = (ep_index * hot_load + order_rank) % host_count
    hot_target = (spread * HOT + which_hot) * spare_slots + order_rank // host_count
    cold_target = (
        flat_ids // exp_dev * primary_slots + flat_ids % exp_dev * capacity + order_rank
    )
    pick_row = jnp.arange(tok_rows * top_count, dtype=jnp.int32) // top_count
    primary_total = ep_count * primary_slots
    spare_total = ep_count * spare_slots
    cold_source = jnp.full((primary_total,), tok_rows, jnp.int32)
    cold_source = cold_source.at[jnp.where(is_hot, primary_total, cold_target)].set(
        pick_row, mode="drop"
    )
    hot_source = jnp.full((spare_total,), tok_rows, jnp.int32)
    hot_source = hot_source.at[jnp.where(is_hot, hot_target, spare_total)].set(
        pick_row, mode="drop"
    )

    slice_width = tokens.shape[1]
    source_row = jnp.concatenate(
        [cold_source.reshape(ep_count, primary_slots), hot_source.reshape(ep_count, spare_slots)],
        axis=1,
    )
    outgoing = jnp.take(tokens, source_row, axis=0, mode="fill", fill_value=0)
    arrived = lax.all_to_all(outgoing, EP, split_axis=0, concat_axis=0, tiled=True)
    incoming = gather_dp(arrived, dp_count)
    primary_rows = incoming[:, :, :primary_slots].reshape(
        dp_count, ep_count, exp_dev, capacity, slice_width
    )
    spare_rows = incoming[:, :, primary_slots:]
    gate_split = gate_weight.reshape(exp_dev, dp_count, slice_width, -1)
    up_split = up_weight.reshape(exp_dev, dp_count, slice_width, -1)

    gate_primary = jnp.einsum(
        "nsecd,endf->secf", primary_rows, gate_split, preferred_element_type=jnp.float32
    )
    up_primary = jnp.einsum(
        "nsecd,endf->secf", primary_rows, up_split, preferred_element_type=jnp.float32
    )
    hidden_primary = silu_product(gate_primary, up_primary)
    part_primary = gather_dp(hidden_primary, dp_count)
    feature_local = down_weight.shape[2]
    down_split = down_weight.reshape(exp_dev, dp_count, -1, feature_local)
    out_primary = jnp.einsum(
        "nsecf,enfd->secd", part_primary, down_split, preferred_element_type=jnp.float32
    ).astype(jnp.bfloat16)

    spare_gate = spare_gate.reshape(dp_count, slice_width, -1)
    spare_up = spare_up.reshape(dp_count, slice_width, -1)
    gate_spare = jnp.einsum(
        "nsrd,ndf->srf", spare_rows, spare_gate, preferred_element_type=jnp.float32
    )
    up_spare = jnp.einsum(
        "nsrd,ndf->srf", spare_rows, spare_up, preferred_element_type=jnp.float32
    )
    hidden_spare = silu_product(gate_spare, up_spare)
    part_spare = gather_dp(hidden_spare, dp_count)
    spare_split = spare_down.reshape(dp_count, -1, feature_local)
    out_spare = jnp.einsum(
        "nsrf,nfd->srd", part_spare, spare_split, preferred_element_type=jnp.float32
    ).astype(jnp.bfloat16)

    per_owner = primary_slots + spare_slots
    results = jnp.concatenate(
        [out_primary.reshape(ep_count, primary_slots, feature_local), out_spare], axis=1
    )
    returned = lax.all_to_all(results, EP, split_axis=0, concat_axis=0, tiled=True).reshape(
        ep_count * per_owner, feature_local
    )
    cold_back = (
        flat_ids // exp_dev * per_owner + flat_ids % exp_dev * capacity + order_rank
    )
    hot_back = (
        hot_target // spare_slots * per_owner + primary_slots + hot_target % spare_slots
    )
    target = jnp.where(is_hot, hot_back, cold_back)
    fetched = jnp.take(returned, target, axis=0).reshape(tok_rows, top_count, feature_local)
    combined = jnp.sum(gate_probs[:, :, None] * fetched.astype(jnp.float32), axis=1)
    return combined.astype(jnp.bfloat16)


def solution(mesh):
    ep_size, dp_size = mesh.devices.shape
    split = Mesh(mesh.devices.reshape(ep_size // HOT, HOT, dp_size), ("eph", "c", "dp"))
    in_specs = (
        P(EP, "dp"),
        P(EP, None),
        P(EP, None),
        P(EP, None, "dp"),
        P(EP, None, "dp"),
        P(EP, None, "dp"),
    )
    out_specs = P(EP, "dp")
    return jax.shard_map(local, mesh=split, in_specs=in_specs, out_specs=out_specs, check_vma=False)
```

```python
import math

import jax
import jax.numpy as jnp
from jax import lax
from jax.sharding import Mesh
from jax.sharding import PartitionSpec as P

HOT = 2
EP = ("eph", "c")


def gather_dp(x, dp_count):
    stacked = jnp.broadcast_to(x[None], (dp_count,) + x.shape)
    return lax.all_to_all(stacked, "dp", split_axis=0, concat_axis=0, tiled=True)


def silu_product(gate_part, up_part):
    return (jax.nn.silu(gate_part) * up_part).astype(jnp.bfloat16)


def local(tokens, expert_ids, gate_probs, gate_weight, up_weight, down_weight):
    pair_count = lax.axis_size("eph")
    ep_count = pair_count * HOT
    dp_count = lax.axis_size("dp")
    parity = lax.axis_index("c")
    ep_index = lax.axis_index("eph") * HOT + parity
    tok_rows, top_count = expert_ids.shape
    exp_dev = gate_weight.shape[0]
    expert_count = exp_dev * ep_count
    hot_load = min(tok_rows * 3 // 4, 4 * tok_rows * top_count // expert_count)
    cold_total = tok_rows * top_count - HOT * hot_load
    capacity = (cold_total + expert_count - HOT - 1) // (expert_count - HOT)
    host_count = pair_count
    spare_slots = max(1, math.ceil(hot_load / host_count))
    primary_slots = exp_dev * capacity

    flat_ids = expert_ids.reshape(-1)
    expert_range = jnp.arange(expert_count, dtype=jnp.int32)
    matches = (flat_ids[:, None] == expert_range[None, :]).astype(jnp.int32)
    expert_loads = jnp.sum(matches, axis=0)
    _, hot_ids = lax.top_k(expert_loads * expert_count + (expert_count - 1 - expert_range), HOT)

    own = (gate_weight[0], up_weight[0], down_weight[0])
    swapped = tuple(lax.ppermute(w, "c", [(0, 1), (1, 0)]) for w in own)
    mine = hot_ids[parity]
    my_expert = ep_index
    sibling_expert = ep_index ^ 1
    take_own = mine == my_expert
    take_sib = mine == sibling_expert
    contrib = tuple(
        jnp.where(take_own, a, jnp.where(take_sib, b, jnp.zeros_like(a)))
        for a, b in zip(own, swapped)
    )
    packed = jnp.concatenate(
        [contrib[0], contrib[1], contrib[2].reshape(-1, contrib[0].shape[1])], axis=0
    )
    blocks = packed.reshape(pair_count, -1, packed.shape[1])

    earlier = jnp.cumsum(matches, axis=0) - matches
    order_rank = jnp.sum(earlier * matches, axis=1)
    hot_match = (flat_ids[:, None] == hot_ids[None, :]).astype(jnp.int32)
    is_hot = jnp.sum(hot_match, axis=1) > 0
    which_hot = jnp.sum(hot_match * jnp.arange(HOT, dtype=jnp.int32)[None, :], axis=1)
    spread = (ep_index * hot_load + order_rank) % host_count
    hot_target = (spread * HOT + which_hot) * spare_slots + order_rank // host_count
    cold_target = (
        flat_ids // exp_dev * primary_slots + flat_ids % exp_dev * capacity + order_rank
    )
    pick_row = jnp.arange(tok_rows * top_count, dtype=jnp.int32) // top_count
    primary_total = ep_count * primary_slots
    spare_total = ep_count * spare_slots
    cold_source = jnp.full((primary_total,), tok_rows, jnp.int32)
    cold_source = cold_source.at[jnp.where(is_hot, primary_total, cold_target)].set(
        pick_row, mode="drop"
    )
    hot_source = jnp.full((spare_total,), tok_rows, jnp.int32)
    hot_source = hot_source.at[jnp.where(is_hot, hot_target, spare_total)].set(
        pick_row, mode="drop"
    )

    slice_width = tokens.shape[1]
    source_row = jnp.concatenate(
        [cold_source.reshape(ep_count, primary_slots), hot_source.reshape(ep_count, spare_slots)],
        axis=1,
    )
    outgoing = jnp.take(tokens, source_row, axis=0, mode="fill", fill_value=0)
    paired = outgoing.reshape(pair_count, HOT, -1, slice_width)
    paired = lax.all_to_all(paired, "c", split_axis=1, concat_axis=1, tiled=True)
    piece_size = blocks.shape[1] * blocks.shape[2]
    merged = jnp.concatenate(
        [blocks.reshape(pair_count, -1), paired.reshape(pair_count, -1)], axis=1
    )
    merged = lax.all_to_all(merged, "eph", split_axis=0, concat_axis=0, tiled=True)
    pieces = merged[:, :piece_size].reshape(blocks.shape)
    arrived = merged[:, piece_size:].reshape(ep_count, -1, slice_width)
    piece = lax.dynamic_index_in_dim(pieces, hot_ids[parity] // HOT, axis=0, keepdims=False)
    spread_back = lax.all_gather(piece, "eph", axis=0, tiled=True)
    model_rows = contrib[0].shape[0]
    spare_gate = spread_back[:model_rows]
    spare_up = spread_back[model_rows : 2 * model_rows]
    spare_down = spread_back[2 * model_rows :].reshape(contrib[2].shape)
    incoming = gather_dp(arrived, dp_count)
    primary_rows = incoming[:, :, :primary_slots].reshape(
        dp_count, ep_count, exp_dev, capacity, slice_width
    )
    spare_rows = incoming[:, :, primary_slots:]
    gate_split = gate_weight.reshape(exp_dev, dp_count, slice_width, -1)
    up_split = up_weight.reshape(exp_dev, dp_count, slice_width, -1)

    gate_primary = jnp.einsum(
        "nsecd,endf->secf", primary_rows, gate_split, preferred_element_type=jnp.float32
    )
    up_primary = jnp.einsum(
        "nsecd,endf->secf", primary_rows, up_split, preferred_element_type=jnp.float32
    )
    hidden_primary = silu_product(gate_primary, up_primary)
    part_primary = gather_dp(hidden_primary, dp_count)
    feature_local = down_weight.shape[2]
    down_split = down_weight.reshape(exp_dev, dp_count, -1, feature_local)
    out_primary = jnp.einsum(
        "nsecf,enfd->secd", part_primary, down_split, preferred_element_type=jnp.float32
    ).astype(jnp.bfloat16)

    spare_gate = spare_gate.reshape(dp_count, slice_width, -1)
    spare_up = spare_up.reshape(dp_count, slice_width, -1)
    gate_spare = jnp.einsum(
        "nsrd,ndf->srf", spare_rows, spare_gate, preferred_element_type=jnp.float32
    )
    up_spare = jnp.einsum(
        "nsrd,ndf->srf", spare_rows, spare_up, preferred_element_type=jnp.float32
    )
    hidden_spare = silu_product(gate_spare, up_spare)
    part_spare = gather_dp(hidden_spare, dp_count)
    spare_split = spare_down.reshape(dp_count, -1, feature_local)
    out_spare = jnp.einsum(
        "nsrf,nfd->srd", part_spare, spare_split, preferred_element_type=jnp.float32
    ).astype(jnp.bfloat16)

    per_owner = primary_slots + spare_slots
    results = jnp.concatenate(
        [out_primary.reshape(ep_count, primary_slots, feature_local), out_spare], axis=1
    )
    returned = lax.all_to_all(results, EP, split_axis=0, concat_axis=0, tiled=True).reshape(
        ep_count * per_owner, feature_local
    )
    cold_back = (
        flat_ids // exp_dev * per_owner + flat_ids % exp_dev * capacity + order_rank
    )
    hot_back = (
        hot_target // spare_slots * per_owner + primary_slots + hot_target % spare_slots
    )
    target = jnp.where(is_hot, hot_back, cold_back)
    fetched = jnp.take(returned, target, axis=0).reshape(tok_rows, top_count, feature_local)
    combined = jnp.sum(gate_probs[:, :, None] * fetched.astype(jnp.float32), axis=1)
    return combined.astype(jnp.bfloat16)


def solution(mesh):
    ep_size, dp_size = mesh.devices.shape
    split = Mesh(mesh.devices.reshape(ep_size // HOT, HOT, dp_size), ("eph", "c", "dp"))
    in_specs = (
        P(EP, "dp"),
        P(EP, None),
        P(EP, None),
        P(EP, None, "dp"),
        P(EP, None, "dp"),
        P(EP, None, "dp"),
    )
    out_specs = P(EP, "dp")
    return jax.shard_map(local, mesh=split, in_specs=in_specs, out_specs=out_specs, check_vma=False)
```

```python
import math

import jax
import jax.numpy as jnp
from jax import lax
from jax.sharding import Mesh
from jax.sharding import PartitionSpec as P

HOT = 2
EP = ("eph", "c")


def gather_dp(x, dp_count):
    stacked = jnp.broadcast_to(x[None], (dp_count,) + x.shape)
    return lax.all_to_all(stacked, "dp", split_axis=0, concat_axis=0, tiled=True)


def silu_product(gate_part, up_part):
    return (jax.nn.silu(gate_part) * up_part).astype(jnp.bfloat16)


def local(tokens, expert_ids, gate_probs, gate_weight, up_weight, down_weight):
    pair_count = lax.axis_size("eph")
    ep_count = pair_count * HOT
    dp_count = lax.axis_size("dp")
    parity = lax.axis_index("c")
    ep_index = lax.axis_index("eph") * HOT + parity
    tok_rows, top_count = expert_ids.shape
    exp_dev = gate_weight.shape[0]
    expert_count = exp_dev * ep_count
    hot_load = min(tok_rows * 3 // 4, 4 * tok_rows * top_count // expert_count)
    cold_total = tok_rows * top_count - HOT * hot_load
    capacity = (cold_total + expert_count - HOT - 1) // (expert_count - HOT)
    host_count = pair_count
    spare_slots = max(1, math.ceil(hot_load / host_count))
    primary_slots = exp_dev * capacity

    flat_ids = expert_ids.reshape(-1)
    expert_range = jnp.arange(expert_count, dtype=jnp.int32)
    matches = (flat_ids[:, None] == expert_range[None, :]).astype(jnp.int32)
    expert_loads = jnp.sum(matches, axis=0)
    _, hot_ids = lax.top_k(expert_loads * expert_count + (expert_count - 1 - expert_range), HOT)

    own = (gate_weight[0], up_weight[0], down_weight[0])
    swapped = tuple(lax.ppermute(w, "c", [(0, 1), (1, 0)]) for w in own)
    mine = hot_ids[parity]
    my_expert = ep_index
    sibling_expert = ep_index ^ 1
    take_own = mine == my_expert
    take_sib = mine == sibling_expert
    contrib = tuple(
        jnp.where(take_own, a, jnp.where(take_sib, b, jnp.zeros_like(a)))
        for a, b in zip(own, swapped)
    )
    packed = jnp.concatenate(
        [contrib[0], contrib[1], contrib[2].reshape(-1, contrib[0].shape[1])], axis=0
    )
    blocks = packed.reshape(pair_count, -1, packed.shape[1])

    earlier = jnp.cumsum(matches, axis=0) - matches
    order_rank = jnp.sum(earlier * matches, axis=1)
    hot_match = (flat_ids[:, None] == hot_ids[None, :]).astype(jnp.int32)
    is_hot = jnp.sum(hot_match, axis=1) > 0
    which_hot = jnp.sum(hot_match * jnp.arange(HOT, dtype=jnp.int32)[None, :], axis=1)
    spread = (ep_index * hot_load + order_rank) % host_count
    hot_target = (spread * HOT + which_hot) * spare_slots + order_rank // host_count
    cold_target = (
        flat_ids // exp_dev * primary_slots + flat_ids % exp_dev * capacity + order_rank
    )
    pick_row = jnp.arange(tok_rows * top_count, dtype=jnp.int32) // top_count
    primary_total = ep_count * primary_slots
    spare_total = ep_count * spare_slots
    cold_source = jnp.full((primary_total,), tok_rows, jnp.int32)
    cold_source = cold_source.at[jnp.where(is_hot, primary_total, cold_target)].set(
        pick_row, mode="drop"
    )
    hot_source = jnp.full((spare_total,), tok_rows, jnp.int32)
    hot_source = hot_source.at[jnp.where(is_hot, hot_target, spare_total)].set(
        pick_row, mode="drop"
    )

    slice_width = tokens.shape[1]
    source_row = jnp.concatenate(
        [cold_source.reshape(ep_count, primary_slots), hot_source.reshape(ep_count, spare_slots)],
        axis=1,
    )
    outgoing = jnp.take(tokens, source_row, axis=0, mode="fill", fill_value=0)
    paired = outgoing.reshape(pair_count, HOT, -1, slice_width)
    paired = lax.all_to_all(paired, "c", split_axis=1, concat_axis=1, tiled=True)
    lane = blocks.shape[2]
    piece_rows = blocks.shape[1]
    merged = jnp.concatenate(
        [blocks, paired.reshape(pair_count, -1, lane)], axis=1
    )
    merged = lax.all_to_all(merged, "eph", split_axis=0, concat_axis=0, tiled=True)
    pieces = merged[:, :piece_rows]
    arrived = merged[:, piece_rows:].reshape(ep_count, -1, slice_width)
    piece = lax.dynamic_index_in_dim(pieces, hot_ids[parity] // HOT, axis=0, keepdims=False)
    spread_back = lax.all_gather(piece, "eph", axis=0, tiled=True)
    model_rows = contrib[0].shape[0]
    spare_gate = spread_back[:model_rows]
    spare_up = spread_back[model_rows : 2 * model_rows]
    spare_down = spread_back[2 * model_rows :].reshape(contrib[2].shape)
    incoming = gather_dp(arrived, dp_count)
    primary_rows = incoming[:, :, :primary_slots].reshape(
        dp_count, ep_count, exp_dev, capacity, slice_width
    )
    spare_rows = incoming[:, :, primary_slots:]
    gate_split = gate_weight.reshape(exp_dev, dp_count, slice_width, -1)
    up_split = up_weight.reshape(exp_dev, dp_count, slice_width, -1)

    gate_primary = jnp.einsum(
        "nsecd,endf->secf", primary_rows, gate_split, preferred_element_type=jnp.float32
    )
    up_primary = jnp.einsum(
        "nsecd,endf->secf", primary_rows, up_split, preferred_element_type=jnp.float32
    )
    hidden_primary = silu_product(gate_primary, up_primary)
    part_primary = gather_dp(hidden_primary, dp_count)
    feature_local = down_weight.shape[2]
    down_split = down_weight.reshape(exp_dev, dp_count, -1, feature_local)
    out_primary = jnp.einsum(
        "nsecf,enfd->secd", part_primary, down_split, preferred_element_type=jnp.float32
    ).astype(jnp.bfloat16)

    spare_gate = spare_gate.reshape(dp_count, slice_width, -1)
    spare_up = spare_up.reshape(dp_count, slice_width, -1)
    gate_spare = jnp.einsum(
        "nsrd,ndf->srf", spare_rows, spare_gate, preferred_element_type=jnp.float32
    )
    up_spare = jnp.einsum(
        "nsrd,ndf->srf", spare_rows, spare_up, preferred_element_type=jnp.float32
    )
    hidden_spare = silu_product(gate_spare, up_spare)
    part_spare = gather_dp(hidden_spare, dp_count)
    spare_split = spare_down.reshape(dp_count, -1, feature_local)
    out_spare = jnp.einsum(
        "nsrf,nfd->srd", part_spare, spare_split, preferred_element_type=jnp.float32
    ).astype(jnp.bfloat16)

    per_owner = primary_slots + spare_slots
    results = jnp.concatenate(
        [out_primary.reshape(ep_count, primary_slots, feature_local), out_spare], axis=1
    )
    returned = lax.all_to_all(results, EP, split_axis=0, concat_axis=0, tiled=True).reshape(
        ep_count * per_owner, feature_local
    )
    cold_back = (
        flat_ids // exp_dev * per_owner + flat_ids % exp_dev * capacity + order_rank
    )
    hot_back = (
        hot_target // spare_slots * per_owner + primary_slots + hot_target % spare_slots
    )
    target = jnp.where(is_hot, hot_back, cold_back)
    fetched = jnp.take(returned, target, axis=0).reshape(tok_rows, top_count, feature_local)
    combined = jnp.sum(gate_probs[:, :, None] * fetched.astype(jnp.float32), axis=1)
    return combined.astype(jnp.bfloat16)


def solution(mesh):
    ep_size, dp_size = mesh.devices.shape
    split = Mesh(mesh.devices.reshape(ep_size // HOT, HOT, dp_size), ("eph", "c", "dp"))
    in_specs = (
        P(EP, "dp"),
        P(EP, None),
        P(EP, None),
        P(EP, None, "dp"),
        P(EP, None, "dp"),
        P(EP, None, "dp"),
    )
    out_specs = P(EP, "dp")
    return jax.shard_map(local, mesh=split, in_specs=in_specs, out_specs=out_specs, check_vma=False)
```

```python
import math

import jax
import jax.numpy as jnp
from jax import lax
from jax.sharding import Mesh
from jax.sharding import PartitionSpec as P

HOT = 2
EP = ("eph", "c")


def gather_dp(x, dp_count):
    stacked = jnp.broadcast_to(x[None], (dp_count,) + x.shape)
    return lax.all_to_all(stacked, "dp", split_axis=0, concat_axis=0, tiled=True)


def silu_product(gate_part, up_part):
    return (jax.nn.silu(gate_part) * up_part).astype(jnp.bfloat16)


def local(tokens, expert_ids, gate_probs, gate_weight, up_weight, down_weight):
    pair_count = lax.axis_size("eph")
    ep_count = pair_count * HOT
    dp_count = lax.axis_size("dp")
    parity = lax.axis_index("c")
    ep_index = lax.axis_index("eph") * HOT + parity
    tok_rows, top_count = expert_ids.shape
    exp_dev = gate_weight.shape[0]
    expert_count = exp_dev * ep_count
    hot_load = min(tok_rows * 3 // 4, 4 * tok_rows * top_count // expert_count)
    cold_total = tok_rows * top_count - HOT * hot_load
    capacity = (cold_total + expert_count - HOT - 1) // (expert_count - HOT)
    host_count = pair_count
    spare_slots = max(1, math.ceil(hot_load / host_count))
    primary_slots = exp_dev * capacity

    flat_ids = expert_ids.reshape(-1)
    expert_range = jnp.arange(expert_count, dtype=jnp.int32)
    matches = (flat_ids[:, None] == expert_range[None, :]).astype(jnp.int32)
    expert_loads = jnp.sum(matches, axis=0)
    _, hot_ids = lax.top_k(expert_loads * expert_count + (expert_count - 1 - expert_range), HOT)

    own = (gate_weight[0], up_weight[0], down_weight[0])
    swapped = tuple(lax.ppermute(w, "c", [(0, 1), (1, 0)]) for w in own)
    mine = hot_ids[parity]
    my_expert = ep_index
    sibling_expert = ep_index ^ 1
    take_own = mine == my_expert
    take_sib = mine == sibling_expert
    contrib = tuple(
        jnp.where(take_own, a, jnp.where(take_sib, b, jnp.zeros_like(a)))
        for a, b in zip(own, swapped)
    )
    packed = jnp.concatenate(
        [contrib[0], contrib[1], contrib[2].reshape(-1, contrib[0].shape[1])], axis=0
    )
    blocks = packed.reshape(pair_count, -1, packed.shape[1])
    pieces = lax.all_to_all(blocks, "eph", split_axis=0, concat_axis=0, tiled=True)
    piece = lax.dynamic_index_in_dim(pieces, hot_ids[parity] // HOT, axis=0, keepdims=False)
    spread_back = lax.all_gather(piece, "eph", axis=0, tiled=True)
    model_rows = contrib[0].shape[0]
    spare_gate = spread_back[:model_rows]
    spare_up = spread_back[model_rows : 2 * model_rows]
    spare_down = spread_back[2 * model_rows :].reshape(contrib[2].shape)
    tokens, contrib = lax.optimization_barrier((tokens, contrib))

    earlier = jnp.cumsum(matches, axis=0) - matches
    order_rank = jnp.sum(earlier * matches, axis=1)
    hot_match = (flat_ids[:, None] == hot_ids[None, :]).astype(jnp.int32)
    is_hot = jnp.sum(hot_match, axis=1) > 0
    which_hot = jnp.sum(hot_match * jnp.arange(HOT, dtype=jnp.int32)[None, :], axis=1)
    spread = (ep_index * hot_load + order_rank) % host_count
    hot_target = (spread * HOT + which_hot) * spare_slots + order_rank // host_count
    cold_target = (
        flat_ids // exp_dev * primary_slots + flat_ids % exp_dev * capacity + order_rank
    )
    pick_row = jnp.arange(tok_rows * top_count, dtype=jnp.int32) // top_count
    primary_total = ep_count * primary_slots
    spare_total = ep_count * spare_slots
    cold_source = jnp.full((primary_total,), tok_rows, jnp.int32)
    cold_source = cold_source.at[jnp.where(is_hot, primary_total, cold_target)].set(
        pick_row, mode="drop"
    )
    hot_source = jnp.full((spare_total,), tok_rows, jnp.int32)
    hot_source = hot_source.at[jnp.where(is_hot, hot_target, spare_total)].set(
        pick_row, mode="drop"
    )

    slice_width = tokens.shape[1]
    source_row = jnp.concatenate(
        [cold_source.reshape(ep_count, primary_slots), hot_source.reshape(ep_count, spare_slots)],
        axis=1,
    )
    outgoing = jnp.take(tokens, source_row, axis=0, mode="fill", fill_value=0)
    arrived = lax.all_to_all(outgoing, EP, split_axis=0, concat_axis=0, tiled=True)
    incoming = gather_dp(arrived, dp_count)
    primary_rows = incoming[:, :, :primary_slots].reshape(
        dp_count, ep_count, exp_dev, capacity, slice_width
    )
    spare_rows = incoming[:, :, primary_slots:]
    gate_split = gate_weight.reshape(exp_dev, dp_count, slice_width, -1)
    up_split = up_weight.reshape(exp_dev, dp_count, slice_width, -1)

    gate_primary = jnp.einsum(
        "nsecd,endf->secf", primary_rows, gate_split, preferred_element_type=jnp.float32
    )
    up_primary = jnp.einsum(
        "nsecd,endf->secf", primary_rows, up_split, preferred_element_type=jnp.float32
    )
    hidden_primary = silu_product(gate_primary, up_primary)
    feature_local = down_weight.shape[2]
    down_split = down_weight.reshape(exp_dev, dp_count, -1, feature_local)

    spare_gate = spare_gate.reshape(dp_count, slice_width, -1)
    spare_up = spare_up.reshape(dp_count, slice_width, -1)
    gate_spare = jnp.einsum(
        "nsrd,ndf->srf", spare_rows, spare_gate, preferred_element_type=jnp.float32
    )
    up_spare = jnp.einsum(
        "nsrd,ndf->srf", spare_rows, spare_up, preferred_element_type=jnp.float32
    )
    hidden_spare = silu_product(gate_spare, up_spare)

    hidden_all = jnp.concatenate(
        [hidden_primary.reshape(ep_count, primary_slots, -1), hidden_spare], axis=1
    )
    part_all = gather_dp(hidden_all, dp_count)
    part_primary = part_all[:, :, :primary_slots].reshape(
        dp_count, ep_count, exp_dev, capacity, -1
    )
    part_spare = part_all[:, :, primary_slots:]
    out_primary = jnp.einsum(
        "nsecf,enfd->secd", part_primary, down_split, preferred_element_type=jnp.float32
    ).astype(jnp.bfloat16)
    spare_split = spare_down.reshape(dp_count, -1, feature_local)
    out_spare = jnp.einsum(
        "nsrf,nfd->srd", part_spare, spare_split, preferred_element_type=jnp.float32
    ).astype(jnp.bfloat16)

    per_owner = primary_slots + spare_slots
    results = jnp.concatenate(
        [out_primary.reshape(ep_count, primary_slots, feature_local), out_spare], axis=1
    )
    returned = lax.all_to_all(results, EP, split_axis=0, concat_axis=0, tiled=True).reshape(
        ep_count * per_owner, feature_local
    )
    cold_back = (
        flat_ids // exp_dev * per_owner + flat_ids % exp_dev * capacity + order_rank
    )
    hot_back = (
        hot_target // spare_slots * per_owner + primary_slots + hot_target % spare_slots
    )
    target = jnp.where(is_hot, hot_back, cold_back)
    fetched = jnp.take(returned, target, axis=0).reshape(tok_rows, top_count, feature_local)
    combined = jnp.sum(gate_probs[:, :, None] * fetched.astype(jnp.float32), axis=1)
    return combined.astype(jnp.bfloat16)


def solution(mesh):
    ep_size, dp_size = mesh.devices.shape
    split = Mesh(mesh.devices.reshape(ep_size // HOT, HOT, dp_size), ("eph", "c", "dp"))
    in_specs = (
        P(EP, "dp"),
        P(EP, None),
        P(EP, None),
        P(EP, None, "dp"),
        P(EP, None, "dp"),
        P(EP, None, "dp"),
    )
    out_specs = P(EP, "dp")
    return jax.shard_map(local, mesh=split, in_specs=in_specs, out_specs=out_specs, check_vma=False)
```

```python
import math

import jax
import jax.numpy as jnp
from jax import lax
from jax.sharding import Mesh
from jax.sharding import PartitionSpec as P

HOT = 2
EP = ("eph", "c")


def gather_dp(x, dp_count):
    stacked = jnp.broadcast_to(x[None], (dp_count,) + x.shape)
    return lax.all_to_all(stacked, "dp", split_axis=0, concat_axis=0, tiled=True)


def silu_product(gate_part, up_part):
    return (jax.nn.silu(gate_part) * up_part).astype(jnp.bfloat16)


def local(tokens, expert_ids, gate_probs, gate_weight, up_weight, down_weight):
    pair_count = lax.axis_size("eph")
    ep_count = pair_count * HOT
    dp_count = lax.axis_size("dp")
    parity = lax.axis_index("c")
    ep_index = lax.axis_index("eph") * HOT + parity
    tok_rows, top_count = expert_ids.shape
    exp_dev = gate_weight.shape[0]
    expert_count = exp_dev * ep_count
    hot_load = min(tok_rows * 3 // 4, 4 * tok_rows * top_count // expert_count)
    cold_total = tok_rows * top_count - HOT * hot_load
    capacity = (cold_total + expert_count - HOT - 1) // (expert_count - HOT)
    host_count = pair_count
    spare_slots = max(1, math.ceil(hot_load / host_count))
    primary_slots = exp_dev * capacity

    flat_ids = expert_ids.reshape(-1)
    expert_range = jnp.arange(expert_count, dtype=jnp.int32)
    matches = (flat_ids[:, None] == expert_range[None, :]).astype(jnp.int32)
    expert_loads = jnp.sum(matches, axis=0)
    _, hot_ids = lax.top_k(expert_loads * expert_count + (expert_count - 1 - expert_range), HOT)

    lane = gate_weight.shape[2]
    own = jnp.concatenate(
        [gate_weight[0], up_weight[0], down_weight[0].reshape(-1, lane)], axis=0
    )
    swapped = lax.ppermute(own, "c", [(0, 1), (1, 0)])
    mine = hot_ids[parity]
    my_expert = ep_index
    sibling_expert = ep_index ^ 1
    take_own = mine == my_expert
    take_sib = mine == sibling_expert
    packed = jnp.where(take_own, own, jnp.where(take_sib, swapped, jnp.zeros_like(own)))
    blocks = packed.reshape(pair_count, -1, packed.shape[1])
    pieces = lax.all_to_all(blocks, "eph", split_axis=0, concat_axis=0, tiled=True)
    piece = lax.dynamic_index_in_dim(pieces, hot_ids[parity] // HOT, axis=0, keepdims=False)
    spread_back = lax.all_gather(piece, "eph", axis=0, tiled=True)
    model_rows = gate_weight.shape[1]
    spare_gate = spread_back[:model_rows]
    spare_up = spread_back[model_rows : 2 * model_rows]
    spare_down = spread_back[2 * model_rows :].reshape(down_weight.shape[1:])
    tokens, packed = lax.optimization_barrier((tokens, packed))

    earlier = jnp.cumsum(matches, axis=0) - matches
    order_rank = jnp.sum(earlier * matches, axis=1)
    hot_match = (flat_ids[:, None] == hot_ids[None, :]).astype(jnp.int32)
    is_hot = jnp.sum(hot_match, axis=1) > 0
    which_hot = jnp.sum(hot_match * jnp.arange(HOT, dtype=jnp.int32)[None, :], axis=1)
    spread = (ep_index * hot_load + order_rank) % host_count
    hot_target = (spread * HOT + which_hot) * spare_slots + order_rank // host_count
    cold_target = (
        flat_ids // exp_dev * primary_slots + flat_ids % exp_dev * capacity + order_rank
    )
    pick_row = jnp.arange(tok_rows * top_count, dtype=jnp.int32) // top_count
    primary_total = ep_count * primary_slots
    spare_total = ep_count * spare_slots
    cold_source = jnp.full((primary_total,), tok_rows, jnp.int32)
    cold_source = cold_source.at[jnp.where(is_hot, primary_total, cold_target)].set(
        pick_row, mode="drop"
    )
    hot_source = jnp.full((spare_total,), tok_rows, jnp.int32)
    hot_source = hot_source.at[jnp.where(is_hot, hot_target, spare_total)].set(
        pick_row, mode="drop"
    )

    slice_width = tokens.shape[1]
    source_row = jnp.concatenate(
        [cold_source.reshape(ep_count, primary_slots), hot_source.reshape(ep_count, spare_slots)],
        axis=1,
    )
    outgoing = jnp.take(tokens, source_row, axis=0, mode="fill", fill_value=0)
    arrived = lax.all_to_all(outgoing, EP, split_axis=0, concat_axis=0, tiled=True)
    incoming = gather_dp(arrived, dp_count)
    primary_rows = incoming[:, :, :primary_slots].reshape(
        dp_count, ep_count, exp_dev, capacity, slice_width
    )
    spare_rows = incoming[:, :, primary_slots:]
    gate_split = gate_weight.reshape(exp_dev, dp_count, slice_width, -1)
    up_split = up_weight.reshape(exp_dev, dp_count, slice_width, -1)

    gate_primary = jnp.einsum(
        "nsecd,endf->secf", primary_rows, gate_split, preferred_element_type=jnp.float32
    )
    up_primary = jnp.einsum(
        "nsecd,endf->secf", primary_rows, up_split, preferred_element_type=jnp.float32
    )
    hidden_primary = silu_product(gate_primary, up_primary)
    part_primary = gather_dp(hidden_primary, dp_count)
    feature_local = down_weight.shape[2]
    down_split = down_weight.reshape(exp_dev, dp_count, -1, feature_local)
    out_primary = jnp.einsum(
        "nsecf,enfd->secd", part_primary, down_split, preferred_element_type=jnp.float32
    ).astype(jnp.bfloat16)

    spare_gate = spare_gate.reshape(dp_count, slice_width, -1)
    spare_up = spare_up.reshape(dp_count, slice_width, -1)
    gate_spare = jnp.einsum(
        "nsrd,ndf->srf", spare_rows, spare_gate, preferred_element_type=jnp.float32
    )
    up_spare = jnp.einsum(
        "nsrd,ndf->srf", spare_rows, spare_up, preferred_element_type=jnp.float32
    )
    hidden_spare = silu_product(gate_spare, up_spare)
    part_spare = gather_dp(hidden_spare, dp_count)
    spare_split = spare_down.reshape(dp_count, -1, feature_local)
    out_spare = jnp.einsum(
        "nsrf,nfd->srd", part_spare, spare_split, preferred_element_type=jnp.float32
    ).astype(jnp.bfloat16)

    per_owner = primary_slots + spare_slots
    results = jnp.concatenate(
        [out_primary.reshape(ep_count, primary_slots, feature_local), out_spare], axis=1
    )
    returned = lax.all_to_all(results, EP, split_axis=0, concat_axis=0, tiled=True).reshape(
        ep_count * per_owner, feature_local
    )
    cold_back = (
        flat_ids // exp_dev * per_owner + flat_ids % exp_dev * capacity + order_rank
    )
    hot_back = (
        hot_target // spare_slots * per_owner + primary_slots + hot_target % spare_slots
    )
    target = jnp.where(is_hot, hot_back, cold_back)
    fetched = jnp.take(returned, target, axis=0).reshape(tok_rows, top_count, feature_local)
    combined = jnp.sum(gate_probs[:, :, None] * fetched.astype(jnp.float32), axis=1)
    return combined.astype(jnp.bfloat16)


def solution(mesh):
    ep_size, dp_size = mesh.devices.shape
    split = Mesh(mesh.devices.reshape(ep_size // HOT, HOT, dp_size), ("eph", "c", "dp"))
    in_specs = (
        P(EP, "dp"),
        P(EP, None),
        P(EP, None),
        P(EP, None, "dp"),
        P(EP, None, "dp"),
        P(EP, None, "dp"),
    )
    out_specs = P(EP, "dp")
    return jax.shard_map(local, mesh=split, in_specs=in_specs, out_specs=out_specs, check_vma=False)
```

```python
import math

import jax
import jax.numpy as jnp
from jax import lax
from jax.sharding import Mesh
from jax.sharding import PartitionSpec as P

HOT = 2
EP = ("eph", "c")


def gather_dp(x, dp_count):
    stacked = jnp.broadcast_to(x[None], (dp_count,) + x.shape)
    return lax.all_to_all(stacked, "dp", split_axis=0, concat_axis=0, tiled=True)


def silu_product(gate_part, up_part):
    return (jax.nn.silu(gate_part) * up_part).astype(jnp.bfloat16)


def local(tokens, expert_ids, gate_probs, gate_weight, up_weight, down_weight):
    pair_count = lax.axis_size("eph")
    ep_count = pair_count * HOT
    dp_count = lax.axis_size("dp")
    parity = lax.axis_index("c")
    ep_index = lax.axis_index("eph") * HOT + parity
    tok_rows, top_count = expert_ids.shape
    exp_dev = gate_weight.shape[0]
    expert_count = exp_dev * ep_count
    hot_load = min(tok_rows * 3 // 4, 4 * tok_rows * top_count // expert_count)
    cold_total = tok_rows * top_count - HOT * hot_load
    capacity = (cold_total + expert_count - HOT - 1) // (expert_count - HOT)
    host_count = pair_count
    spare_slots = max(1, math.ceil(hot_load / host_count))
    primary_slots = exp_dev * capacity

    flat_ids = expert_ids.reshape(-1)
    expert_range = jnp.arange(expert_count, dtype=jnp.int32)
    matches = (flat_ids[:, None] == expert_range[None, :]).astype(jnp.int32)
    expert_loads = jnp.sum(matches, axis=0)
    _, hot_ids = lax.top_k(expert_loads * expert_count + (expert_count - 1 - expert_range), HOT)

    lane = gate_weight.shape[2]
    own = jnp.concatenate(
        [gate_weight[0], up_weight[0], down_weight[0].reshape(-1, lane)], axis=0
    )
    swapped = lax.ppermute(own, "c", [(0, 1), (1, 0)])
    mine = hot_ids[parity]
    my_expert = ep_index
    sibling_expert = ep_index ^ 1
    take_own = mine == my_expert
    take_sib = mine == sibling_expert
    packed = jnp.where(take_own, own, jnp.where(take_sib, swapped, jnp.zeros_like(own)))
    earlier = jnp.cumsum(matches, axis=0) - matches
    order_rank = jnp.sum(earlier * matches, axis=1)
    hot_match = (flat_ids[:, None] == hot_ids[None, :]).astype(jnp.int32)
    is_hot = jnp.sum(hot_match, axis=1) > 0
    which_hot = jnp.sum(hot_match * jnp.arange(HOT, dtype=jnp.int32)[None, :], axis=1)
    spread = (ep_index * hot_load + order_rank) % host_count
    hot_target = (spread * HOT + which_hot) * spare_slots + order_rank // host_count
    cold_target = (
        flat_ids // exp_dev * primary_slots + flat_ids % exp_dev * capacity + order_rank
    )
    pick_row = jnp.arange(tok_rows * top_count, dtype=jnp.int32) // top_count
    primary_total = ep_count * primary_slots
    spare_total = ep_count * spare_slots
    cold_source = jnp.full((primary_total,), tok_rows, jnp.int32)
    cold_source = cold_source.at[jnp.where(is_hot, primary_total, cold_target)].set(
        pick_row, mode="drop"
    )
    hot_source = jnp.full((spare_total,), tok_rows, jnp.int32)
    hot_source = hot_source.at[jnp.where(is_hot, hot_target, spare_total)].set(
        pick_row, mode="drop"
    )

    slice_width = tokens.shape[1]
    source_row = jnp.concatenate(
        [cold_source.reshape(ep_count, primary_slots), hot_source.reshape(ep_count, spare_slots)],
        axis=1,
    )
    outgoing = jnp.take(tokens, source_row, axis=0, mode="fill", fill_value=0)
    arrived = lax.all_to_all(outgoing, EP, split_axis=0, concat_axis=0, tiled=True)
    arrived, packed = lax.optimization_barrier((arrived, packed))
    blocks = packed.reshape(pair_count, -1, packed.shape[1])
    pieces = lax.all_to_all(blocks, "eph", split_axis=0, concat_axis=0, tiled=True)
    piece = lax.dynamic_index_in_dim(pieces, hot_ids[parity] // HOT, axis=0, keepdims=False)
    spread_back = lax.all_gather(piece, "eph", axis=0, tiled=True)
    model_rows = gate_weight.shape[1]
    spare_gate = spread_back[:model_rows]
    spare_up = spread_back[model_rows : 2 * model_rows]
    spare_down = spread_back[2 * model_rows :].reshape(down_weight.shape[1:])

    arrived, piece = lax.optimization_barrier((arrived, piece))
    incoming = gather_dp(arrived, dp_count)
    primary_rows = incoming[:, :, :primary_slots].reshape(
        dp_count, ep_count, exp_dev, capacity, slice_width
    )
    spare_rows = incoming[:, :, primary_slots:]
    gate_split = gate_weight.reshape(exp_dev, dp_count, slice_width, -1)
    up_split = up_weight.reshape(exp_dev, dp_count, slice_width, -1)

    gate_primary = jnp.einsum(
        "nsecd,endf->secf", primary_rows, gate_split, preferred_element_type=jnp.float32
    )
    up_primary = jnp.einsum(
        "nsecd,endf->secf", primary_rows, up_split, preferred_element_type=jnp.float32
    )
    hidden_primary = silu_product(gate_primary, up_primary)
    part_primary = gather_dp(hidden_primary, dp_count)
    feature_local = down_weight.shape[2]
    down_split = down_weight.reshape(exp_dev, dp_count, -1, feature_local)
    out_primary = jnp.einsum(
        "nsecf,enfd->secd", part_primary, down_split, preferred_element_type=jnp.float32
    ).astype(jnp.bfloat16)

    spare_gate = spare_gate.reshape(dp_count, slice_width, -1)
    spare_up = spare_up.reshape(dp_count, slice_width, -1)
    gate_spare = jnp.einsum(
        "nsrd,ndf->srf", spare_rows, spare_gate, preferred_element_type=jnp.float32
    )
    up_spare = jnp.einsum(
        "nsrd,ndf->srf", spare_rows, spare_up, preferred_element_type=jnp.float32
    )
    hidden_spare = silu_product(gate_spare, up_spare)
    part_spare = gather_dp(hidden_spare, dp_count)
    spare_split = spare_down.reshape(dp_count, -1, feature_local)
    out_spare = jnp.einsum(
        "nsrf,nfd->srd", part_spare, spare_split, preferred_element_type=jnp.float32
    ).astype(jnp.bfloat16)

    per_owner = primary_slots + spare_slots
    results = jnp.concatenate(
        [out_primary.reshape(ep_count, primary_slots, feature_local), out_spare], axis=1
    )
    returned = lax.all_to_all(results, EP, split_axis=0, concat_axis=0, tiled=True).reshape(
        ep_count * per_owner, feature_local
    )
    cold_back = (
        flat_ids // exp_dev * per_owner + flat_ids % exp_dev * capacity + order_rank
    )
    hot_back = (
        hot_target // spare_slots * per_owner + primary_slots + hot_target % spare_slots
    )
    target = jnp.where(is_hot, hot_back, cold_back)
    fetched = jnp.take(returned, target, axis=0).reshape(tok_rows, top_count, feature_local)
    combined = jnp.sum(gate_probs[:, :, None] * fetched.astype(jnp.float32), axis=1)
    return combined.astype(jnp.bfloat16)


def solution(mesh):
    ep_size, dp_size = mesh.devices.shape
    split = Mesh(mesh.devices.reshape(ep_size // HOT, HOT, dp_size), ("eph", "c", "dp"))
    in_specs = (
        P(EP, "dp"),
        P(EP, None),
        P(EP, None),
        P(EP, None, "dp"),
        P(EP, None, "dp"),
        P(EP, None, "dp"),
    )
    out_specs = P(EP, "dp")
    return jax.shard_map(local, mesh=split, in_specs=in_specs, out_specs=out_specs, check_vma=False)
```

```python
import math

import jax
import jax.numpy as jnp
from jax import lax
from jax.sharding import Mesh
from jax.sharding import PartitionSpec as P

HOT = 2
EP = ("eph", "c")


def gather_dp(x, dp_count):
    stacked = jnp.broadcast_to(x[None], (dp_count,) + x.shape)
    return lax.all_to_all(stacked, "dp", split_axis=0, concat_axis=0, tiled=True)


def silu_product(gate_part, up_part):
    return (jax.nn.silu(gate_part) * up_part).astype(jnp.bfloat16)


def local(tokens, expert_ids, gate_probs, gate_weight, up_weight, down_weight):
    pair_count = lax.axis_size("eph")
    ep_count = pair_count * HOT
    dp_count = lax.axis_size("dp")
    parity = lax.axis_index("c")
    ep_index = lax.axis_index("eph") * HOT + parity
    tok_rows, top_count = expert_ids.shape
    exp_dev = gate_weight.shape[0]
    expert_count = exp_dev * ep_count
    hot_load = min(tok_rows * 3 // 4, 4 * tok_rows * top_count // expert_count)
    cold_total = tok_rows * top_count - HOT * hot_load
    capacity = (cold_total + expert_count - HOT - 1) // (expert_count - HOT)
    host_count = pair_count
    spare_slots = max(1, math.ceil(hot_load / host_count))
    primary_slots = exp_dev * capacity

    flat_ids = expert_ids.reshape(-1)
    expert_range = jnp.arange(expert_count, dtype=jnp.int32)
    matches = (flat_ids[:, None] == expert_range[None, :]).astype(jnp.int32)
    expert_loads = jnp.sum(matches, axis=0)
    _, hot_ids = lax.top_k(expert_loads * expert_count + (expert_count - 1 - expert_range), HOT)

    lane = gate_weight.shape[2]
    own = jnp.concatenate(
        [gate_weight[0], up_weight[0], down_weight[0].reshape(-1, lane)], axis=0
    )
    swapped = lax.ppermute(own, "c", [(0, 1), (1, 0)])
    mine = hot_ids[parity]
    my_expert = ep_index
    sibling_expert = ep_index ^ 1
    take_own = mine == my_expert
    take_sib = mine == sibling_expert
    packed = jnp.where(take_own, own, jnp.where(take_sib, swapped, jnp.zeros_like(own)))
    blocks = packed.reshape(pair_count, -1, packed.shape[1])
    pieces = lax.all_to_all(blocks, "eph", split_axis=0, concat_axis=0, tiled=True)
    piece = lax.dynamic_index_in_dim(pieces, hot_ids[parity] // HOT, axis=0, keepdims=False)
    spread_back = lax.all_gather(piece, "eph", axis=0, tiled=True)
    model_rows = gate_weight.shape[1]
    spare_gate = spread_back[:model_rows]
    spare_up = spread_back[model_rows : 2 * model_rows]
    spare_down = spread_back[2 * model_rows :].reshape(down_weight.shape[1:])

    earlier = jnp.cumsum(matches, axis=0) - matches
    order_rank = jnp.sum(earlier * matches, axis=1)
    hot_match = (flat_ids[:, None] == hot_ids[None, :]).astype(jnp.int32)
    is_hot = jnp.sum(hot_match, axis=1) > 0
    which_hot = jnp.sum(hot_match * jnp.arange(HOT, dtype=jnp.int32)[None, :], axis=1)
    spread = (ep_index * hot_load + order_rank) % host_count
    hot_target = (spread * HOT + which_hot) * spare_slots + order_rank // host_count
    cold_target = (
        flat_ids // exp_dev * primary_slots + flat_ids % exp_dev * capacity + order_rank
    )
    pick_row = jnp.arange(tok_rows * top_count, dtype=jnp.int32) // top_count
    primary_total = ep_count * primary_slots
    spare_total = ep_count * spare_slots
    cold_source = jnp.full((primary_total,), tok_rows, jnp.int32)
    cold_source = cold_source.at[jnp.where(is_hot, primary_total, cold_target)].set(
        pick_row, mode="drop"
    )
    hot_source = jnp.full((spare_total,), tok_rows, jnp.int32)
    hot_source = hot_source.at[jnp.where(is_hot, hot_target, spare_total)].set(
        pick_row, mode="drop"
    )

    slice_width = tokens.shape[1]
    source_row = jnp.concatenate(
        [cold_source.reshape(ep_count, primary_slots), hot_source.reshape(ep_count, spare_slots)],
        axis=1,
    )
    outgoing = jnp.take(tokens, source_row, axis=0, mode="fill", fill_value=0)
    arrived = lax.all_to_all(outgoing, EP, split_axis=0, concat_axis=0, tiled=True)
    incoming = gather_dp(arrived, dp_count)
    primary_rows = incoming[:, :, :primary_slots].reshape(
        dp_count, ep_count, exp_dev, capacity, slice_width
    )
    spare_rows = incoming[:, :, primary_slots:]
    gate_split = gate_weight.reshape(exp_dev, dp_count, slice_width, -1)
    up_split = up_weight.reshape(exp_dev, dp_count, slice_width, -1)

    gate_primary = jnp.einsum(
        "nsecd,endf->secf", primary_rows, gate_split, preferred_element_type=jnp.float32
    )
    up_primary = jnp.einsum(
        "nsecd,endf->secf", primary_rows, up_split, preferred_element_type=jnp.float32
    )
    hidden_primary = silu_product(gate_primary, up_primary)
    part_primary = gather_dp(hidden_primary, dp_count)
    feature_local = down_weight.shape[2]
    down_split = down_weight.reshape(exp_dev, dp_count, -1, feature_local)
    out_primary = jnp.einsum(
        "nsecf,enfd->secd", part_primary, down_split, preferred_element_type=jnp.float32
    ).astype(jnp.bfloat16)

    spare_gate = spare_gate.reshape(dp_count, slice_width, -1)
    spare_up = spare_up.reshape(dp_count, slice_width, -1)
    gate_spare = jnp.einsum(
        "nsrd,ndf->srf", spare_rows, spare_gate, preferred_element_type=jnp.float32
    )
    up_spare = jnp.einsum(
        "nsrd,ndf->srf", spare_rows, spare_up, preferred_element_type=jnp.float32
    )
    hidden_spare = silu_product(gate_spare, up_spare)
    part_spare = gather_dp(hidden_spare, dp_count)
    spare_split = spare_down.reshape(dp_count, -1, feature_local)
    out_spare = jnp.einsum(
        "nsrf,nfd->srd", part_spare, spare_split, preferred_element_type=jnp.float32
    ).astype(jnp.bfloat16)

    per_owner = primary_slots + spare_slots
    results = jnp.concatenate(
        [out_primary.reshape(ep_count, primary_slots, feature_local), out_spare], axis=1
    )
    returned = lax.all_to_all(results, EP, split_axis=0, concat_axis=0, tiled=True).reshape(
        ep_count * per_owner, feature_local
    )
    cold_back = (
        flat_ids // exp_dev * per_owner + flat_ids % exp_dev * capacity + order_rank
    )
    hot_back = (
        hot_target // spare_slots * per_owner + primary_slots + hot_target % spare_slots
    )
    target = jnp.where(is_hot, hot_back, cold_back)
    fetched = jnp.take(returned, target, axis=0).reshape(tok_rows, top_count, feature_local)
    combined = jnp.sum(gate_probs[:, :, None] * fetched.astype(jnp.float32), axis=1)
    return combined.astype(jnp.bfloat16)


def solution(mesh):
    ep_size, dp_size = mesh.devices.shape
    split = Mesh(mesh.devices.reshape(ep_size // HOT, HOT, dp_size), ("eph", "c", "dp"))
    in_specs = (
        P(EP, "dp"),
        P(EP, None),
        P(EP, None),
        P(EP, None, "dp"),
        P(EP, None, "dp"),
        P(EP, None, "dp"),
    )
    out_specs = P(EP, "dp")
    return jax.shard_map(local, mesh=split, in_specs=in_specs, out_specs=out_specs, check_vma=False)
```
